512 devices in a mesh: lon: 16 (over x_hi, y), lat: 16 (over z, core), segment: 2 (over x_lo).
Axes of the slice: x: 4 (x_hi: 2, x_lo: 2; x = x_hi * 2 + x_lo), y: 8, z: 8, core: 2. Of those that a mesh axis runs over, the one named last changes fastest.
Arguments:
- initial_state: float32 [2, 32, 64, 8, 384], P(None, 'lat', 'lon'), may hold values from -6 to 6
- mask_ids: int32 [32, 64], P('lat', 'lon'), may hold values from 0 to 7
- lead_steps: int32 [2], replicated, may hold values from 0 to 7, as said below
- mask_table: float32 [2, 8, 384], P('segment'), may hold values from -3 to 3
- lead_table: float32 [2, 8, 384], P('segment'), may hold values from -3 to 3
- w_qkv: bfloat16 [2, 384, 1152], P('segment'), may hold values from -0.3125 to 0.3125
- w_out: bfloat16 [2, 384, 384], P('segment'), may hold values from -0.3125 to 0.3125
- w_up: bfloat16 [2, 384, 1536], P('segment'), may hold values from -0.3125 to 0.3125
- w_down: bfloat16 [2, 1536, 384], P('segment'), may hold values from -0.15625 to 0.15625
- norm_gains: float32 [2, 3, 384], P('segment'), may hold values from 0.5 to 1.5
- merid_taps: float32 [2, 5, 384], P('segment'), may hold values from -1.5 to 1.5
- score_bias: float32 [2, 12, 8, 64], P('segment'), may hold values from -4 to 250
Outputs:
- forecasts: float32 [2, 2, 32, 64, 8, 384], P('segment', None, 'lat', 'lon')
The draws below stay inside these ranges and needn't reach their ends.
Inputs may be any that keep to these rules, and one draw needn't show every extreme that they name: `lead_steps`: the two rollout steps have different lead-time classes.
All inputs are finite; a program needn't handle non-finite values.
Results may differ from the reference program's by a relative error of at most 0.012.
Values may be sent and summed in bfloat16 or wider, within the bound.
No kernel may reach another device: no remote copies, remote signals or barrier semaphores. Data moves between devices by JAX's collectives and lax.ppermute only.
A program may use at most 64 MiB of HBM per device.

```python
import jax
import jax.numpy as jnp
from jax import lax

C = 384
HEADS = 12
FF = 1536
HEAD_DIM = 32
MEMBERS = 2
LEV = 8
MASK_KINDS = 8
LEADS = 8
LAT = 32
LON = 64


def draw_lead_steps(key, part):
    first_key, step_key = jax.random.split(jax.random.fold_in(key, 7), 2)
    first_class = jax.random.randint(first_key, (), 0, LEADS).astype(jnp.int32)
    advance = jax.random.randint(step_key, (), 1, LEADS).astype(jnp.int32)
    second_class = jnp.mod(first_class + advance, LEADS).astype(jnp.int32)
    return jnp.stack([first_class, second_class]).astype(jnp.int32)


def draw_score_bias(key, part):
    base_key = jax.random.fold_in(key, 0)
    base = jnp.clip(jax.random.normal(base_key, (2, HEADS, LEV, LON), jnp.float32), -4.0, 4.0)
    return base


def place_ends(values, rng, smallest, top_value):
    longest = values.shape.index(max(values.shape))
    spots = []
    for shift in (0, 1):
        where = [jax.random.randint(jax.random.fold_in(rng, axis), (), 0, length) for axis, length in enumerate(values.shape)]
        where[longest] = (where[longest] + shift) % values.shape[longest]
        spots.append(tuple(where))
    return values.at[spots[0]].set(smallest).at[spots[1]].set(top_value)


def level_of(key, extent, cuts, smallest, high):
    def one(dim, shards_of):
        draws = jax.random.uniform(jax.random.fold_in(jax.random.fold_in(key, 6), dim), (shards_of,), jnp.float32, smallest / len(cuts), high / len(cuts))
        return jnp.repeat(jnp.exp(draws), extent[dim] // shards_of).reshape((-1,) + (1,) * (len(extent) - dim - 1))

    loudness = one(*cuts[0])
    for cut in cuts[1:]:
        loudness = loudness * one(*cut)
    return loudness


def scatter_about(key, dims, width, reach, pieces=(), kind=jnp.bfloat16):
    drawn = width * jax.random.normal(key, dims, jnp.float32)
    if pieces:
        drawn = drawn * level_of(key, dims, pieces, -0.22, 0.18)
    return jnp.clip(drawn, -reach, reach).astype(kind)


def setup_inputs(seed: int = 0) -> dict:
    seeds = jax.random.split(jax.random.key(seed), 13)
    initial_state = scatter_about(seeds[0], (MEMBERS, LAT, LON, LEV, C), 1.0, 6.0, ((1, 16), (2, 16)), jnp.float32)
    mask_ids = place_ends(jax.random.randint(seeds[1], (LAT, LON), 0, MASK_KINDS), jax.random.fold_in(seeds[1], 1), 0, MASK_KINDS - 1).astype(jnp.int32)
    lead_steps = draw_lead_steps(jax.random.fold_in(seeds[12], 71), 0)
    mask_table = scatter_about(seeds[3], (2, MASK_KINDS, C), 0.5, 3.0, ((0, 2),), jnp.float32)
    lead_table = scatter_about(seeds[4], (2, LEADS, C), 0.5, 3.0, ((0, 2),), jnp.float32)
    w_qkv = scatter_about(seeds[5], (2, C, 3 * C), C ** -0.5, 0.3125, ((0, 2),))
    w_out = scatter_about(seeds[6], (2, C, C), C ** -0.5, 0.3125, ((0, 2),))
    w_up = scatter_about(seeds[7], (2, C, FF), C ** -0.5, 0.3125, ((0, 2),))
    w_down = scatter_about(seeds[8], (2, FF, C), FF ** -0.5, 0.15625, ((0, 2),))
    norm_gains = jnp.clip(1.0 + 0.1 * jax.random.normal(seeds[9], (2, 3, C), jnp.float32), 0.5, 1.5)
    merid_taps = scatter_about(seeds[10], (2, 5, C), 0.3, 1.5, ((0, 2),), jnp.float32)
    score_bias = draw_score_bias(jax.random.fold_in(seeds[12], 71), 0)
    return dict(initial_state=initial_state, mask_ids=mask_ids, lead_steps=lead_steps, mask_table=mask_table, lead_table=lead_table, w_qkv=w_qkv, w_out=w_out, w_up=w_up, w_down=w_down, norm_gains=norm_gains, merid_taps=merid_taps, score_bias=score_bias)


epsilon = 1e-05

def layer_norm(values, gain_row):
    mean_val = lax.optimization_barrier(jnp.mean(values, axis=-1, keepdims=True))
    centered = values - mean_val
    variance = lax.optimization_barrier(jnp.mean(centered * centered, axis=-1, keepdims=True))
    return centered * lax.rsqrt(variance + epsilon) * gain_row

def bias_table(bias_segment, query_start, query_count, key_start, key_count, lon_total):
    query_lon = query_start + jnp.arange(query_count, dtype=jnp.int32)
    key_lon = key_start + jnp.arange(key_count, dtype=jnp.int32)
    offsets = jnp.mod(key_lon[None, :] - query_lon[:, None], lon_total).astype(jnp.int32)
    picked = jnp.take(bias_segment, offsets, axis=2)
    picked = jnp.transpose(picked, (0, 2, 1, 3))
    head_count, levels = (bias_segment.shape[0], bias_segment.shape[1])
    picked = jnp.broadcast_to(picked[..., None], (head_count, query_count, levels, key_count, levels))
    return picked.reshape(head_count, query_count * levels, key_count * levels)

def segment_block(field_in, lead_index, mask_ids, mask_tab, lead_tab, wqkv, wout, wup, wdown, gains, taps, bias_segment):
    mask_onehot = (mask_ids[..., None] == jnp.arange(MASK_KINDS, dtype=jnp.int32)).astype(jnp.float32)
    mask_embed = jnp.dot(mask_onehot, mask_tab, precision=lax.Precision.HIGHEST)
    lead_onehot = (lead_index == jnp.arange(LEADS, dtype=jnp.int32)).astype(jnp.float32)
    lead_row = jnp.dot(lead_onehot, lead_tab, precision=lax.Precision.HIGHEST)
    hidden = field_in + mask_embed[:, :, None, :] + lead_row
    normed = layer_norm(hidden, gains[0]).astype(jnp.bfloat16)
    projected = jnp.dot(normed.reshape(-1, C), wqkv, preferred_element_type=jnp.float32).astype(jnp.bfloat16)
    projected = projected.reshape(LAT, LON * LEV, 3, HEADS, HEAD_DIM)
    bias_full = bias_table(bias_segment, 0, LON, 0, LON, LON)
    score_scale = HEAD_DIM ** (-0.5)

    def one_row(row_parts):
        query_rows, key_rows, value_rows = row_parts
        scores = jnp.einsum('qhd,khd->hqk', query_rows.astype(jnp.float32), key_rows.astype(jnp.float32)) * score_scale + bias_full
        row_max = lax.optimization_barrier(jnp.max(scores, axis=-1, keepdims=True))
        weights = jnp.exp(scores - row_max)
        total = lax.optimization_barrier(jnp.sum(weights, axis=-1))
        rounded = weights.astype(jnp.bfloat16).astype(jnp.float32)
        summed = jnp.einsum('hqk,khd->hqd', rounded, value_rows.astype(jnp.float32))
        result = summed / total[..., None]
        return jnp.transpose(result, (1, 0, 2))
    attended = lax.map(one_row, (projected[:, :, 0], projected[:, :, 1], projected[:, :, 2]))
    mixed = attended.reshape(-1, C).astype(jnp.bfloat16)
    hidden2 = hidden + jnp.dot(mixed, wout, preferred_element_type=jnp.float32).reshape(hidden.shape)
    normed2 = layer_norm(hidden2, gains[1]).astype(jnp.bfloat16)
    padded = jnp.pad(normed2, ((2, 2), (0, 0), (0, 0), (0, 0)))
    window_sum = jnp.zeros_like(hidden2)
    for offset_row in range(5):
        window_sum = window_sum + taps[offset_row] * padded[offset_row:offset_row + LAT].astype(jnp.float32)
    hidden3 = hidden2 + window_sum
    normed3 = layer_norm(hidden3, gains[2]).astype(jnp.bfloat16)
    activated = jax.nn.gelu(jnp.dot(normed3.reshape(-1, C), wup, preferred_element_type=jnp.float32), approximate=True).astype(jnp.bfloat16)
    return hidden3 + jnp.dot(activated, wdown, preferred_element_type=jnp.float32).reshape(hidden.shape)

def reference(initial_state, mask_ids, lead_steps, mask_table, lead_table, w_qkv, w_out, w_up, w_down, norm_gains, merid_taps, score_bias):

    def run(field_in, section, rollout):
        return segment_block(field_in, lead_steps[rollout], mask_ids, mask_table[section], lead_table[section], w_qkv[section], w_out[section], w_up[section], w_down[section], norm_gains[section], merid_taps[section], score_bias[section])
    firsts = []
    seconds = []
    for member in range(MEMBERS):
        first = run(run(initial_state[member], 0, 0), 1, 0)
        second = run(run(first, 0, 1), 1, 1)
        firsts.append(first)
        seconds.append(second)
    return jnp.stack([jnp.stack(firsts), jnp.stack(seconds)])
```

```python
import jax
import jax.numpy as jnp
from jax import lax
from jax.sharding import PartitionSpec as P

epsilon = 1e-05


def layer_norm(values, gain_row):
    mean_val = jnp.mean(values, axis=-1, keepdims=True)
    centered = values - mean_val
    variance = jnp.mean(centered * centered, axis=-1, keepdims=True)
    return centered * lax.rsqrt(variance + epsilon) * gain_row


def lat_halo(array, width):
    devices, length = lax.axis_size("lat"), array.shape[1]
    up = [(i, i + 1) for i in range(devices - 1)]
    down = [(j, i) for i, j in up]
    before = lax.ppermute(array[:, length - width :], "lat", up)
    after = lax.ppermute(array[:, :width], "lat", down)
    return jnp.concatenate([before, array, after], axis=1)


def head_bias(bias_segment, groups, lon_total):
    heads_here = bias_segment.shape[0] // groups
    group = lax.axis_index("lon") % groups
    picked = lax.dynamic_slice_in_dim(bias_segment, group * heads_here, heads_here, axis=0)
    lon = jnp.arange(lon_total, dtype=jnp.int32)
    offsets = jnp.mod(lon[None, :] - lon[:, None], lon_total)
    onehot = (offsets[..., None] == lon[None, None, :]).astype(jnp.float32)
    return jnp.einsum("hlo,ijo->hilj", picked, onehot, precision=lax.Precision.HIGHEST)


def block(field, lead_index, mask_ids, params, bias4):
    mask_tab, lead_tab, wqkv, wout, wup, wdown, gains, taps = params
    members, rows_lat, lon_local, levels, features = field.shape
    lon_devices = lax.axis_size("lon")
    head_count = bias4.shape[0] * lon_devices // (members * rows_lat)
    head_dim = features // head_count
    groups = head_count // bias4.shape[0]
    heads_here = bias4.shape[0]
    lon_total = lon_local * lon_devices
    tokens_local = lon_local * levels

    mask_embed = jnp.take(mask_tab, mask_ids, axis=0)
    lead_row = lax.dynamic_index_in_dim(lead_tab, lead_index, axis=0, keepdims=False)
    hidden = field + mask_embed[None, :, :, None, :] + lead_row
    normed = layer_norm(hidden, gains[0]).astype(jnp.bfloat16)
    projected = jnp.dot(
        normed.reshape(-1, features), wqkv, preferred_element_type=jnp.float32
    ).astype(jnp.bfloat16)
    projected = projected.reshape(
        members, rows_lat, tokens_local, 3, groups, heads_here, head_dim
    )
    outgoing = jnp.transpose(projected, (0, 1, 4, 2, 3, 5, 6)).reshape(
        lon_devices, tokens_local, 3, heads_here, head_dim
    )
    incoming = lax.all_to_all(outgoing, "lon", 0, 0, tiled=True)
    incoming = incoming.reshape(lon_total * levels, 3, heads_here, head_dim)
    queries, keys, values = incoming[:, 0], incoming[:, 1], incoming[:, 2]
    scores = jnp.einsum(
        "qhd,khd->hqk", queries, keys, preferred_element_type=jnp.float32
    ) * (head_dim ** (-0.5))
    scores = scores.reshape(heads_here, lon_total, levels, lon_total, levels)
    scores = scores + bias4[..., None]
    scores = scores.reshape(heads_here, lon_total * levels, lon_total * levels)
    row_max = jnp.max(scores, axis=-1, keepdims=True)
    weights = jnp.exp(scores - row_max)
    total = jnp.sum(weights, axis=-1, keepdims=True)
    summed = jnp.einsum(
        "hqk,khd->hqd", weights.astype(jnp.bfloat16), values, preferred_element_type=jnp.float32
    )
    attended = (summed / total).astype(jnp.bfloat16)
    back = jnp.transpose(attended.reshape(heads_here, lon_devices, tokens_local, head_dim), (1, 2, 0, 3))
    returned = lax.all_to_all(back, "lon", 0, 0, tiled=True)
    returned = returned.reshape(members, rows_lat, groups, tokens_local, heads_here, head_dim)
    mixed = jnp.transpose(returned, (0, 1, 3, 2, 4, 5)).reshape(-1, features)
    hidden2 = hidden + jnp.dot(mixed, wout, preferred_element_type=jnp.float32).reshape(hidden.shape)
    normed2 = layer_norm(hidden2, gains[1]).astype(jnp.bfloat16)
    padded = lat_halo(normed2, 2)
    window_sum = jnp.zeros_like(hidden2)
    for offset_row in range(5):
        window_sum = window_sum + taps[offset_row] * padded[:, offset_row : offset_row + rows_lat].astype(
            jnp.float32
        )
    hidden3 = hidden2 + window_sum
    normed3 = layer_norm(hidden3, gains[2]).astype(jnp.bfloat16)
    activated = jax.nn.gelu(
        jnp.dot(normed3.reshape(-1, features), wup, preferred_element_type=jnp.float32),
        approximate=True,
    ).astype(jnp.bfloat16)
    return hidden3 + jnp.dot(activated, wdown, preferred_element_type=jnp.float32).reshape(hidden.shape)


def from_partner(array):
    return lax.ppermute(array, "segment", [(i, i ^ 1) for i in range(lax.axis_size("segment"))])


def body(
    initial_state,
    mask_ids,
    lead_steps,
    mask_table,
    lead_table,
    w_qkv,
    w_out,
    w_up,
    w_down,
    norm_gains,
    merid_taps,
    score_bias,
):
    members, rows_lat = initial_state.shape[0], initial_state.shape[1]
    lon_local = initial_state.shape[2]
    lon_devices = lax.axis_size("lon")
    head_count = score_bias.shape[1]
    groups = lon_devices // (members * rows_lat)
    params = tuple(
        item[0] for item in (mask_table, lead_table, w_qkv, w_out, w_up, w_down, norm_gains, merid_taps)
    )
    bias4 = head_bias(score_bias[0], groups, lon_local * lon_devices)
    segment_first = lax.axis_index("segment") == 0
    current = initial_state
    first = None
    for tick_num in range(4):
        result = block(current, lead_steps[tick_num // 2], mask_ids, params, bias4)
        if tick_num == 3:
            break
        current = from_partner(result)
        if tick_num == 1:
            first = current
    output = jnp.where(segment_first, first, result)
    return output[None]


def solution(mesh):
    in_specs = (
        P(None, "lat", "lon", None, None),
        P("lat", "lon"),
        P(),
        P("segment", None, None),
        P("segment", None, None),
        P("segment", None, None),
        P("segment", None, None),
        P("segment", None, None),
        P("segment", None, None),
        P("segment", None, None),
        P("segment", None, None),
        P("segment", None, None, None),
    )
    out_specs = P("segment", None, "lat", "lon", None, None)
    return jax.shard_map(body, mesh=mesh, in_specs=in_specs, out_specs=out_specs, check_vma=False)
```

```python
import jax
import jax.numpy as jnp
from jax import lax
from jax.sharding import PartitionSpec as P

epsilon = 1e-05


def layer_norm(values, gain_row):
    mean_val = jnp.mean(values, axis=-1, keepdims=True)
    centered = values - mean_val
    variance = jnp.mean(centered * centered, axis=-1, keepdims=True)
    return centered * lax.rsqrt(variance + epsilon) * gain_row


def lat_halo(array, width):
    devices, length = lax.axis_size("lat"), array.shape[1]
    up = [(i, i + 1) for i in range(devices - 1)]
    down = [(j, i) for i, j in up]
    before = lax.ppermute(array[:, length - width :], "lat", up)
    after = lax.ppermute(array[:, :width], "lat", down)
    return jnp.concatenate([before, array, after], axis=1)


def head_bias(bias_segment, groups, lon_total, levels):
    heads_here = bias_segment.shape[0] // groups
    group = lax.axis_index("lon") // (lax.axis_size("lon") // groups)
    picked = lax.dynamic_slice_in_dim(bias_segment, group * heads_here, heads_here, axis=0)
    lhs = picked.reshape(heads_here * levels, lon_total)
    high = lhs.astype(jnp.bfloat16)
    rest = lhs - high.astype(jnp.float32)
    middle = rest.astype(jnp.bfloat16)
    low = (rest - middle.astype(jnp.float32)).astype(jnp.bfloat16)
    lon = jnp.arange(lon_total, dtype=jnp.int32)
    key_lon = jnp.repeat(lon, levels)
    offsets = jnp.mod(key_lon[None, :] - lon[:, None], lon_total)
    onehot = (lon[:, None, None] == offsets[None]).astype(jnp.bfloat16).reshape(lon_total, -1)
    parts = [
        jnp.dot(part, onehot, preferred_element_type=jnp.float32) for part in (high, middle, low)
    ]
    table = (parts[0] + parts[1]) + parts[2]
    table = table.reshape(heads_here, levels, lon_total, lon_total * levels)
    table = jnp.transpose(table, (0, 2, 1, 3))
    return table.reshape(heads_here, lon_total * levels, lon_total * levels)


def block(field, lead_index, mask_ids, params, bias_full):
    mask_tab, lead_tab, wqkv, wout, wup, wdown, gains, taps = params
    members, rows_lat, lon_local, levels, features = field.shape
    groups, _, group_width = wqkv.shape
    heads_here = bias_full.shape[0]
    head_dim = group_width // (3 * heads_here)
    lon_devices = lax.axis_size("lon")
    tokens_local = lon_local * levels
    combos = members * rows_lat

    mask_embed = jnp.take(mask_tab, mask_ids, axis=0)
    lead_row = lax.dynamic_index_in_dim(lead_tab, lead_index, axis=0, keepdims=False)
    hidden = field + mask_embed[None, :, :, None, :] + lead_row
    normed = layer_norm(hidden, gains[0]).astype(jnp.bfloat16)
    spread = jnp.broadcast_to(normed.reshape(1, -1, features), (groups, combos * tokens_local, features))
    projected = jnp.einsum(
        "gnc,gcf->gnf", spread, wqkv, preferred_element_type=jnp.float32
    ).astype(jnp.bfloat16)
    outgoing = projected.reshape(lon_devices, tokens_local, group_width)
    incoming = lax.all_to_all(outgoing, "lon", 0, 0, tiled=True)
    incoming = incoming.reshape(lon_devices * tokens_local, 3, heads_here, head_dim)
    queries, keys, values = incoming[:, 0], incoming[:, 1], incoming[:, 2]
    scores = jnp.einsum(
        "qhd,khd->hqk", queries, keys, preferred_element_type=jnp.float32
    ) * (head_dim ** (-0.5)) + bias_full
    row_max = jnp.max(scores, axis=-1, keepdims=True)
    weights = jnp.exp(scores - row_max)
    total = jnp.sum(weights, axis=-1, keepdims=True)
    summed = jnp.einsum(
        "hqk,khd->hqd", weights.astype(jnp.bfloat16), values, preferred_element_type=jnp.float32
    )
    attended = (summed / total).astype(jnp.bfloat16)
    back = jnp.transpose(attended, (1, 0, 2)).reshape(lon_devices, tokens_local, heads_here * head_dim)
    returned = lax.all_to_all(back, "lon", 0, 0, tiled=True)
    returned = returned.reshape(groups, combos * tokens_local, heads_here * head_dim)
    projected_out = jnp.einsum("gnf,gfo->no", returned, wout, preferred_element_type=jnp.float32)
    hidden2 = hidden + projected_out.reshape(hidden.shape)
    normed2 = layer_norm(hidden2, gains[1]).astype(jnp.bfloat16)
    padded = lat_halo(normed2, 2)
    window_sum = jnp.zeros_like(hidden2)
    for offset_row in range(5):
        window_sum = window_sum + taps[offset_row] * padded[:, offset_row : offset_row + rows_lat].astype(
            jnp.float32
        )
    hidden3 = hidden2 + window_sum
    normed3 = layer_norm(hidden3, gains[2]).astype(jnp.bfloat16)
    activated = jax.nn.gelu(
        jnp.dot(normed3.reshape(-1, features), wup, preferred_element_type=jnp.float32),
        approximate=True,
    ).astype(jnp.bfloat16)
    return hidden3 + jnp.dot(activated, wdown, preferred_element_type=jnp.float32).reshape(hidden.shape)


def from_partner(array):
    return lax.ppermute(array, "segment", [(i, i ^ 1) for i in range(lax.axis_size("segment"))])


def body(
    initial_state,
    mask_ids,
    lead_steps,
    mask_table,
    lead_table,
    w_qkv,
    w_out,
    w_up,
    w_down,
    norm_gains,
    merid_taps,
    score_bias,
):
    members, rows_lat = initial_state.shape[0], initial_state.shape[1]
    lon_local = initial_state.shape[2]
    lon_devices = lax.axis_size("lon")
    head_count = score_bias.shape[1]
    groups = lon_devices // (members * rows_lat)
    mask_tab, lead_tab, wqkv, wout, wup, wdown, gains, taps = tuple(
        item[0] for item in (mask_table, lead_table, w_qkv, w_out, w_up, w_down, norm_gains, merid_taps)
    )
    features = wqkv.shape[0]
    head_dim = features // head_count
    heads_here = head_count // groups
    wqkv = jnp.transpose(wqkv.reshape(features, 3, groups, heads_here * head_dim), (2, 0, 1, 3))
    wqkv = wqkv.reshape(groups, features, 3 * heads_here * head_dim)
    wout = wout.reshape(groups, heads_here * head_dim, features)
    params = (mask_tab, lead_tab, wqkv, wout, wup, wdown, gains, taps)
    bias_full = head_bias(score_bias[0], groups, lon_local * lon_devices, initial_state.shape[3])
    segment_first = lax.axis_index("segment") == 0
    current = initial_state
    first = None
    for tick_num in range(4):
        result = block(current, lead_steps[tick_num // 2], mask_ids, params, bias_full)
        if tick_num == 3:
            break
        current = from_partner(result)
        if tick_num == 1:
            first = current
    output = jnp.where(segment_first, first, result)
    return output[None]


def solution(mesh):
    in_specs = (
        P(None, "lat", "lon", None, None),
        P("lat", "lon"),
        P(),
        P("segment", None, None),
        P("segment", None, None),
        P("segment", None, None),
        P("segment", None, None),
        P("segment", None, None),
        P("segment", None, None),
        P("segment", None, None),
        P("segment", None, None),
        P("segment", None, None, None),
    )
    out_specs = P("segment", None, "lat", "lon", None, None)
    return jax.shard_map(body, mesh=mesh, in_specs=in_specs, out_specs=out_specs, check_vma=False)
```

```python
import functools

import jax
import jax.numpy as jnp
from jax import lax
from jax.experimental import pallas as pl
from jax.experimental.pallas import tpu as pltpu
from jax.sharding import PartitionSpec as P

epsilon = 1e-05


def layer_norm(values, gain_row):
    mean_val = jnp.mean(values, axis=-1, keepdims=True)
    centered = values - mean_val
    variance = jnp.mean(centered * centered, axis=-1, keepdims=True)
    return centered * lax.rsqrt(variance + epsilon) * gain_row


def lat_halo(array, width):
    devices, length = lax.axis_size("lat"), array.shape[1]
    up = [(i, i + 1) for i in range(devices - 1)]
    down = [(j, i) for i, j in up]
    before = lax.ppermute(array[:, length - width :], "lat", up)
    after = lax.ppermute(array[:, :width], "lat", down)
    return jnp.concatenate([before, array, after], axis=1)


def head_bias(bias_segment, groups, lon_total, levels):
    heads_here = bias_segment.shape[0] // groups
    group = lax.axis_index("lon") // (lax.axis_size("lon") // groups)
    picked = lax.dynamic_slice_in_dim(bias_segment, group * heads_here, heads_here, axis=0)
    lhs = picked.reshape(heads_here * levels, lon_total)
    high = lhs.astype(jnp.bfloat16)
    rest = lhs - high.astype(jnp.float32)
    middle = rest.astype(jnp.bfloat16)
    low = (rest - middle.astype(jnp.float32)).astype(jnp.bfloat16)
    lon = jnp.arange(lon_total, dtype=jnp.int32)
    key_lon = jnp.repeat(lon, levels)
    offsets = jnp.mod(key_lon[None, :] - lon[:, None], lon_total)
    onehot = (lon[:, None, None] == offsets[None]).astype(jnp.bfloat16).reshape(lon_total, -1)
    parts = [
        jnp.dot(part, onehot, preferred_element_type=jnp.float32) for part in (high, middle, low)
    ]
    table = (parts[0] + parts[1]) + parts[2]
    table = table.reshape(heads_here, levels, lon_total, lon_total * levels)
    table = jnp.transpose(table, (0, 2, 1, 3))
    return table.reshape(heads_here, lon_total * levels, lon_total * levels)


def attention_kernel(x_ref, bias_ref, o_ref, *, heads, head_dim):
    width = heads * head_dim
    for h in range(heads):
        cols = slice(h * head_dim, (h + 1) * head_dim)
        q = x_ref[:, cols]
        k = x_ref[:, width + h * head_dim : width + (h + 1) * head_dim]
        v = x_ref[:, 2 * width + h * head_dim : 2 * width + (h + 1) * head_dim]
        s = lax.dot_general(q, k, (((1,), (1,)), ((), ())), preferred_element_type=jnp.float32)
        s = s * (head_dim ** (-0.5)) + bias_ref[h]
        row_max = jnp.max(s, axis=-1, keepdims=True)
        weights = jnp.exp(s - row_max)
        total = jnp.sum(weights, axis=-1, keepdims=True)
        summed = jnp.dot(weights.astype(jnp.bfloat16), v, preferred_element_type=jnp.float32)
        o_ref[:, cols] = (summed / total).astype(o_ref.dtype)


def attend(x, bias_full, head_dim):
    heads = bias_full.shape[0]
    return pl.pallas_call(
        functools.partial(attention_kernel, heads=heads, head_dim=head_dim),
        out_shape=jax.ShapeDtypeStruct((x.shape[0], heads * head_dim), jnp.bfloat16),
        in_specs=[pl.BlockSpec(memory_space=pltpu.VMEM)] * 2,
        out_specs=pl.BlockSpec(memory_space=pltpu.VMEM),
    )(x, bias_full)


def block(field, lead_index, mask_ids, params, bias_full):
    mask_tab, lead_tab, wqkv, wout, wup, wdown, gains, taps = params
    members, rows_lat, lon_local, levels, features = field.shape
    groups, _, group_width = wqkv.shape
    heads_here = bias_full.shape[0]
    head_dim = group_width // (3 * heads_here)
    lon_devices = lax.axis_size("lon")
    tokens_local = lon_local * levels
    combos = members * rows_lat

    mask_embed = jnp.take(mask_tab, mask_ids, axis=0)
    lead_row = lax.dynamic_index_in_dim(lead_tab, lead_index, axis=0, keepdims=False)
    hidden = field + mask_embed[None, :, :, None, :] + lead_row
    normed = layer_norm(hidden, gains[0]).astype(jnp.bfloat16)
    spread = jnp.broadcast_to(normed.reshape(1, -1, features), (groups, combos * tokens_local, features))
    projected = jnp.einsum(
        "gnc,gcf->gnf", spread, wqkv, preferred_element_type=jnp.float32
    ).astype(jnp.bfloat16)
    outgoing = projected.reshape(lon_devices, tokens_local, group_width)
    incoming = lax.all_to_all(outgoing, "lon", 0, 0, tiled=True)
    attended = attend(incoming.reshape(lon_devices * tokens_local, group_width), bias_full, head_dim)
    back = attended.reshape(lon_devices, tokens_local, heads_here * head_dim)
    returned = lax.all_to_all(back, "lon", 0, 0, tiled=True)
    returned = returned.reshape(groups, combos * tokens_local, heads_here * head_dim)
    projected_out = jnp.einsum("gnf,gfo->no", returned, wout, preferred_element_type=jnp.float32)
    hidden2 = hidden + projected_out.reshape(hidden.shape)
    normed2 = layer_norm(hidden2, gains[1]).astype(jnp.bfloat16)
    padded = lat_halo(normed2, 2)
    window_sum = jnp.zeros_like(hidden2)
    for offset_row in range(5):
        window_sum = window_sum + taps[offset_row] * padded[:, offset_row : offset_row + rows_lat].astype(
            jnp.float32
        )
    hidden3 = hidden2 + window_sum
    normed3 = layer_norm(hidden3, gains[2]).astype(jnp.bfloat16)
    activated = jax.nn.gelu(
        jnp.dot(normed3.reshape(-1, features), wup, preferred_element_type=jnp.float32),
        approximate=True,
    ).astype(jnp.bfloat16)
    return hidden3 + jnp.dot(activated, wdown, preferred_element_type=jnp.float32).reshape(hidden.shape)


def from_partner(array):
    return lax.ppermute(array, "segment", [(i, i ^ 1) for i in range(lax.axis_size("segment"))])


def body(
    initial_state,
    mask_ids,
    lead_steps,
    mask_table,
    lead_table,
    w_qkv,
    w_out,
    w_up,
    w_down,
    norm_gains,
    merid_taps,
    score_bias,
):
    members, rows_lat = initial_state.shape[0], initial_state.shape[1]
    lon_local = initial_state.shape[2]
    lon_devices = lax.axis_size("lon")
    head_count = score_bias.shape[1]
    groups = lon_devices // (members * rows_lat)
    mask_tab, lead_tab, wqkv, wout, wup, wdown, gains, taps = tuple(
        item[0] for item in (mask_table, lead_table, w_qkv, w_out, w_up, w_down, norm_gains, merid_taps)
    )
    features = wqkv.shape[0]
    head_dim = features // head_count
    heads_here = head_count // groups
    wqkv = jnp.transpose(wqkv.reshape(features, 3, groups, heads_here * head_dim), (2, 0, 1, 3))
    wqkv = wqkv.reshape(groups, features, 3 * heads_here * head_dim)
    wout = wout.reshape(groups, heads_here * head_dim, features)
    params = (mask_tab, lead_tab, wqkv, wout, wup, wdown, gains, taps)
    bias_full = head_bias(score_bias[0], groups, lon_local * lon_devices, initial_state.shape[3])
    segment_first = lax.axis_index("segment") == 0
    current = initial_state
    first = None
    for tick_num in range(4):
        result = block(current, lead_steps[tick_num // 2], mask_ids, params, bias_full)
        if tick_num == 3:
            break
        current = from_partner(result)
        if tick_num == 1:
            first = current
    output = jnp.where(segment_first, first, result)
    return output[None]


def solution(mesh):
    in_specs = (
        P(None, "lat", "lon", None, None),
        P("lat", "lon"),
        P(),
        P("segment", None, None),
        P("segment", None, None),
        P("segment", None, None),
        P("segment", None, None),
        P("segment", None, None),
        P("segment", None, None),
        P("segment", None, None),
        P("segment", None, None),
        P("segment", None, None, None),
    )
    out_specs = P("segment", None, "lat", "lon", None, None)
    return jax.shard_map(body, mesh=mesh, in_specs=in_specs, out_specs=out_specs, check_vma=False)
```

```python
import functools

import jax
import jax.numpy as jnp
from jax import lax
from jax.experimental import pallas as pl
from jax.experimental.pallas import tpu as pltpu
from jax.sharding import PartitionSpec as P

epsilon = 1e-05


def layer_norm(values, gain_row):
    mean_val = jnp.mean(values, axis=-1, keepdims=True)
    centered = values - mean_val
    variance = jnp.mean(centered * centered, axis=-1, keepdims=True)
    return centered * lax.rsqrt(variance + epsilon) * gain_row


def lat_halo(array, width):
    devices, length = lax.axis_size("lat"), array.shape[1]
    up = [(i, i + 1) for i in range(devices - 1)]
    down = [(j, i) for i, j in up]
    before = lax.ppermute(array[:, length - width :], "lat", up)
    after = lax.ppermute(array[:, :width], "lat", down)
    return jnp.concatenate([before, array, after], axis=1)


def head_bias(bias_segment, groups, lon_total, levels):
    heads_here = bias_segment.shape[0] // groups
    group = lax.axis_index("lon") // (lax.axis_size("lon") // groups)
    picked = lax.dynamic_slice_in_dim(bias_segment, group * heads_here, heads_here, axis=0)
    lhs = picked.reshape(heads_here * levels, lon_total)
    high = lhs.astype(jnp.bfloat16)
    rest = lhs - high.astype(jnp.float32)
    middle = rest.astype(jnp.bfloat16)
    low = (rest - middle.astype(jnp.float32)).astype(jnp.bfloat16)
    lon = jnp.arange(lon_total, dtype=jnp.int32)
    key_lon = jnp.repeat(lon, levels)
    offsets = jnp.mod(key_lon[None, :] - lon[:, None], lon_total)
    onehot = (lon[:, None, None] == offsets[None]).astype(jnp.bfloat16).reshape(lon_total, -1)
    parts = [
        jnp.dot(part, onehot, preferred_element_type=jnp.float32) for part in (high, middle, low)
    ]
    table = (parts[0] + parts[1]) + parts[2]
    table = table.reshape(heads_here, levels, lon_total, lon_total * levels)
    table = jnp.transpose(table, (0, 2, 1, 3))
    return table.reshape(heads_here, lon_total * levels, lon_total * levels)


def attention_kernel(x_ref, bias_ref, o_ref, *, heads, head_dim):
    width = heads * head_dim
    for h in range(heads):
        cols = slice(h * head_dim, (h + 1) * head_dim)
        q = x_ref[:, cols]
        k = x_ref[:, width + h * head_dim : width + (h + 1) * head_dim]
        v = x_ref[:, 2 * width + h * head_dim : 2 * width + (h + 1) * head_dim]
        s = lax.dot_general(q, k, (((1,), (1,)), ((), ())), preferred_element_type=jnp.float32)
        s = s * (head_dim ** (-0.5)) + bias_ref[h]
        row_max = jnp.max(s, axis=-1, keepdims=True)
        weights = jnp.exp(s - row_max)
        total = jnp.sum(weights, axis=-1, keepdims=True)
        summed = jnp.dot(weights.astype(jnp.bfloat16), v, preferred_element_type=jnp.float32)
        o_ref[:, cols] = (summed / total).astype(o_ref.dtype)


def attend(x, bias_full, head_dim):
    heads = bias_full.shape[0]
    return pl.pallas_call(
        functools.partial(attention_kernel, heads=heads, head_dim=head_dim),
        out_shape=jax.ShapeDtypeStruct((x.shape[0], heads * head_dim), jnp.bfloat16),
        in_specs=[pl.BlockSpec(memory_space=pltpu.VMEM)] * 2,
        out_specs=pl.BlockSpec(memory_space=pltpu.VMEM),
    )(x, bias_full)


def block(field, lead_index, mask_ids, params, bias_full):
    mask_tab, lead_tab, wqkv, wout, wup, wdown, gains, taps = params
    members, rows_lat, lon_local, levels, features = field.shape
    groups, _, group_width = wqkv.shape
    heads_here = bias_full.shape[0]
    head_dim = group_width // (3 * heads_here)
    lon_devices = lax.axis_size("lon")
    tokens_local = lon_local * levels
    combos = members * rows_lat

    mask_embed = jnp.take(mask_tab, mask_ids, axis=0)
    lead_row = lax.dynamic_index_in_dim(lead_tab, lead_index, axis=0, keepdims=False)
    hidden = field + mask_embed[None, :, :, None, :] + lead_row
    normed = layer_norm(hidden, gains[0]).astype(jnp.bfloat16)
    spread = jnp.broadcast_to(normed.reshape(1, -1, features), (groups, combos * tokens_local, features))
    projected = jnp.einsum(
        "gnc,gcf->gnf", spread, wqkv, preferred_element_type=jnp.float32
    ).astype(jnp.bfloat16)
    outgoing = projected.reshape(lon_devices, tokens_local, group_width)
    incoming = lax.all_to_all(outgoing, "lon", 0, 0, tiled=True)
    attended = attend(incoming.reshape(lon_devices * tokens_local, group_width), bias_full, head_dim)
    back = attended.reshape(lon_devices, tokens_local, heads_here * head_dim)
    returned = lax.all_to_all(back, "lon", 0, 0, tiled=True)
    returned = returned.reshape(groups, combos * tokens_local, heads_here * head_dim)
    projected_out = jnp.einsum("gnf,gfo->no", returned, wout, preferred_element_type=jnp.float32)
    hidden2 = hidden + projected_out.reshape(hidden.shape)
    normed2 = layer_norm(hidden2, gains[1]).astype(jnp.bfloat16)
    padded = lat_halo(normed2, 2)
    window_sum = jnp.zeros_like(hidden2)
    for offset_row in range(5):
        window_sum = window_sum + taps[offset_row] * padded[:, offset_row : offset_row + rows_lat].astype(
            jnp.float32
        )
    hidden3 = hidden2 + window_sum
    normed3 = layer_norm(hidden3, gains[2]).astype(jnp.bfloat16)
    activated = jax.nn.gelu(
        jnp.dot(normed3.reshape(-1, features), wup, preferred_element_type=jnp.float32),
        approximate=True,
    ).astype(jnp.bfloat16)
    return hidden3 + jnp.dot(activated, wdown, preferred_element_type=jnp.float32).reshape(hidden.shape)


def from_partner(array):
    return lax.ppermute(array, "segment", [(i, i ^ 1) for i in range(lax.axis_size("segment"))])


def fetch_split(array):
    lat_devices = lax.axis_size("lat")
    core = lax.axis_index("lat") % 2
    half = array.shape[0] // 2
    mine = lax.dynamic_slice_in_dim(array, core * half, half, axis=0)
    got = from_partner(mine)
    neighbour = lax.ppermute(got, "lat", [(i, i ^ 1) for i in range(lat_devices)])
    low = jnp.where(core == 0, got, neighbour)
    high = jnp.where(core == 0, neighbour, got)
    return jnp.concatenate([low, high], axis=0)


def body(
    initial_state,
    mask_ids,
    lead_steps,
    mask_table,
    lead_table,
    w_qkv,
    w_out,
    w_up,
    w_down,
    norm_gains,
    merid_taps,
    score_bias,
):
    members, rows_lat = initial_state.shape[0], initial_state.shape[1]
    lon_local = initial_state.shape[2]
    lon_devices = lax.axis_size("lon")
    head_count = score_bias.shape[1]
    groups = lon_devices // (members * rows_lat)
    own_raw = tuple(
        item[0] for item in (mask_table, lead_table, w_qkv, w_out, w_up, w_down, norm_gains, merid_taps)
    )
    other_raw = tuple(
        fetch_split(item) if item.dtype == jnp.bfloat16 else from_partner(item) for item in own_raw
    )
    other_bias = from_partner(score_bias[0])
    levels = initial_state.shape[3]

    def prepare(raw, bias_segment):
        mask_tab, lead_tab, wqkv, wout, wup, wdown, gains, taps = raw
        features = wqkv.shape[0]
        head_dim = features // head_count
        heads_here = head_count // groups
        wqkv = jnp.transpose(wqkv.reshape(features, 3, groups, heads_here * head_dim), (2, 0, 1, 3))
        wqkv = wqkv.reshape(groups, features, 3 * heads_here * head_dim)
        wout = wout.reshape(groups, heads_here * head_dim, features)
        params = (mask_tab, lead_tab, wqkv, wout, wup, wdown, gains, taps)
        return params, head_bias(bias_segment, groups, lon_local * lon_devices, levels)

    own = prepare(own_raw, score_bias[0])
    other = prepare(other_raw, other_bias)
    segment_first = lax.axis_index("segment") == 0
    out0 = block(initial_state, lead_steps[0], mask_ids, *own)
    first = block(out0, lead_steps[0], mask_ids, *other)
    out2 = block(from_partner(first), lead_steps[1], mask_ids, *other)
    second = block(out2, lead_steps[1], mask_ids, *own)
    output = jnp.where(segment_first, first, second)
    return output[None]


def solution(mesh):
    in_specs = (
        P(None, "lat", "lon", None, None),
        P("lat", "lon"),
        P(),
        P("segment", None, None),
        P("segment", None, None),
        P("segment", None, None),
        P("segment", None, None),
        P("segment", None, None),
        P("segment", None, None),
        P("segment", None, None),
        P("segment", None, None),
        P("segment", None, None, None),
    )
    out_specs = P("segment", None, "lat", "lon", None, None)
    return jax.shard_map(body, mesh=mesh, in_specs=in_specs, out_specs=out_specs, check_vma=False)
```

```python
import functools

import jax
import jax.numpy as jnp
from jax import lax
from jax.experimental import pallas as pl
from jax.experimental.pallas import tpu as pltpu
from jax.sharding import PartitionSpec as P

epsilon = 1e-05


def layer_norm(values, gain_row):
    mean_val = jnp.mean(values, axis=-1, keepdims=True)
    centered = values - mean_val
    variance = jnp.mean(centered * centered, axis=-1, keepdims=True)
    return centered * lax.rsqrt(variance + epsilon) * gain_row


def lat_halo(array, width):
    devices, length = lax.axis_size("lat"), array.shape[1]
    up = [(i, i + 1) for i in range(devices - 1)]
    down = [(j, i) for i, j in up]
    before = lax.ppermute(array[:, length - width :], "lat", up)
    after = lax.ppermute(array[:, :width], "lat", down)
    return jnp.concatenate([before, array, after], axis=1)


def head_bias(bias_segment, groups, lon_total, levels):
    heads_here = bias_segment.shape[0] // groups
    group = lax.axis_index("lon") // (lax.axis_size("lon") // groups)
    picked = lax.dynamic_slice_in_dim(bias_segment, group * heads_here, heads_here, axis=0)
    lhs = picked.reshape(heads_here * levels, lon_total)
    high = lhs.astype(jnp.bfloat16)
    rest = lhs - high.astype(jnp.float32)
    middle = rest.astype(jnp.bfloat16)
    low = (rest - middle.astype(jnp.float32)).astype(jnp.bfloat16)
    lon = jnp.arange(lon_total, dtype=jnp.int32)
    key_lon = jnp.repeat(lon, levels)
    offsets = jnp.mod(key_lon[None, :] - lon[:, None], lon_total)
    onehot = (lon[:, None, None] == offsets[None]).astype(jnp.bfloat16).reshape(lon_total, -1)
    parts = [
        jnp.dot(part, onehot, preferred_element_type=jnp.float32) for part in (high, middle, low)
    ]
    table = (parts[0] + parts[1]) + parts[2]
    table = table.reshape(heads_here, levels, lon_total, lon_total * levels)
    table = jnp.transpose(table, (0, 2, 1, 3))
    return table.reshape(heads_here, lon_total * levels, lon_total * levels)


def attention_kernel(x_ref, bias_ref, o_ref, *, heads, head_dim):
    width = heads * head_dim
    for h in range(heads):
        cols = slice(h * head_dim, (h + 1) * head_dim)
        q = x_ref[:, cols]
        k = x_ref[:, width + h * head_dim : width + (h + 1) * head_dim]
        v = x_ref[:, 2 * width + h * head_dim : 2 * width + (h + 1) * head_dim]
        s = lax.dot_general(q, k, (((1,), (1,)), ((), ())), preferred_element_type=jnp.float32)
        s = s * (head_dim ** (-0.5)) + bias_ref[h]
        row_max = jnp.max(s, axis=-1, keepdims=True)
        weights = jnp.exp(s - row_max)
        total = jnp.sum(weights, axis=-1, keepdims=True)
        summed = jnp.dot(weights.astype(jnp.bfloat16), v, preferred_element_type=jnp.float32)
        o_ref[:, cols] = (summed / total).astype(o_ref.dtype)


def attend(x, bias_full, head_dim):
    heads = bias_full.shape[0]
    return pl.pallas_call(
        functools.partial(attention_kernel, heads=heads, head_dim=head_dim),
        out_shape=jax.ShapeDtypeStruct((x.shape[0], heads * head_dim), jnp.bfloat16),
        in_specs=[pl.BlockSpec(memory_space=pltpu.VMEM)] * 2,
        out_specs=pl.BlockSpec(memory_space=pltpu.VMEM),
    )(x, bias_full)


def block(field, lead_index, mask_ids, params, bias_full):
    mask_tab, lead_tab, wqkv, wout, wup, wdown, gains, taps = params
    members, rows_lat, lon_local, levels, features = field.shape
    groups, _, group_width = wqkv.shape
    heads_here = bias_full.shape[0]
    head_dim = group_width // (3 * heads_here)
    lon_devices = lax.axis_size("lon")
    tokens_local = lon_local * levels
    combos = members * rows_lat

    mask_embed = jnp.take(mask_tab, mask_ids, axis=0)
    lead_row = lax.dynamic_index_in_dim(lead_tab, lead_index, axis=0, keepdims=False)
    hidden = field + mask_embed[None, :, :, None, :] + lead_row
    normed = layer_norm(hidden, gains[0]).astype(jnp.bfloat16)
    spread = jnp.broadcast_to(normed.reshape(1, -1, features), (groups, combos * tokens_local, features))
    projected = jnp.einsum(
        "gnc,gcf->gnf", spread, wqkv, preferred_element_type=jnp.float32
    ).astype(jnp.bfloat16)
    outgoing = projected.reshape(lon_devices, tokens_local, group_width)
    incoming = lax.all_to_all(outgoing, "lon", 0, 0, tiled=True)
    attended = attend(incoming.reshape(lon_devices * tokens_local, group_width), bias_full, head_dim)
    back = attended.reshape(lon_devices, tokens_local, heads_here * head_dim)
    returned = lax.all_to_all(back, "lon", 0, 0, tiled=True)
    returned = returned.reshape(groups, combos * tokens_local, heads_here * head_dim)
    projected_out = jnp.einsum("gnf,gfo->no", returned, wout, preferred_element_type=jnp.float32)
    hidden2 = hidden + projected_out.reshape(hidden.shape)
    normed2 = layer_norm(hidden2, gains[1]).astype(jnp.bfloat16)
    padded = lat_halo(normed2, 2)
    window_sum = jnp.zeros_like(hidden2)
    for offset_row in range(5):
        window_sum = window_sum + taps[offset_row] * padded[:, offset_row : offset_row + rows_lat].astype(
            jnp.float32
        )
    hidden3 = hidden2 + window_sum
    normed3 = layer_norm(hidden3, gains[2]).astype(jnp.bfloat16)
    activated = jax.nn.gelu(
        jnp.dot(normed3.reshape(-1, features), wup, preferred_element_type=jnp.float32),
        approximate=True,
    ).astype(jnp.bfloat16)
    return hidden3 + jnp.dot(activated, wdown, preferred_element_type=jnp.float32).reshape(hidden.shape)


def from_partner(array):
    return lax.ppermute(array, "segment", [(i, i ^ 1) for i in range(lax.axis_size("segment"))])


def body(
    initial_state,
    mask_ids,
    lead_steps,
    mask_table,
    lead_table,
    w_qkv,
    w_out,
    w_up,
    w_down,
    norm_gains,
    merid_taps,
    score_bias,
):
    members, rows_lat = initial_state.shape[0], initial_state.shape[1]
    lon_local = initial_state.shape[2]
    lon_devices = lax.axis_size("lon")
    head_count = score_bias.shape[1]
    groups = lon_devices // (members * rows_lat)
    mask_tab, lead_tab, wqkv, wout, wup, wdown, gains, taps = tuple(
        item[0] for item in (mask_table, lead_table, w_qkv, w_out, w_up, w_down, norm_gains, merid_taps)
    )
    features = wqkv.shape[0]
    head_dim = features // head_count
    heads_here = head_count // groups
    wqkv = jnp.transpose(wqkv.reshape(features, 3, groups, heads_here * head_dim), (2, 0, 1, 3))
    wqkv = wqkv.reshape(groups, features, 3 * heads_here * head_dim)
    wout = wout.reshape(groups, heads_here * head_dim, features)
    params = (mask_tab, lead_tab, wqkv, wout, wup, wdown, gains, taps)
    bias_full = head_bias(score_bias[0], groups, lon_local * lon_devices, initial_state.shape[3])
    segment_first = lax.axis_index("segment") == 0
    current = initial_state
    first = None
    for tick_num in range(4):
        result = lax.cond(
            lax.axis_index("segment") == tick_num % 2,
            lambda state: block(state, lead_steps[tick_num // 2], mask_ids, params, bias_full),
            lambda state: state,
            current,
        )
        if tick_num == 3:
            break
        current = from_partner(result)
        if tick_num == 1:
            first = current
    output = jnp.where(segment_first, first, result)
    return output[None]


def solution(mesh):
    in_specs = (
        P(None, "lat", "lon", None, None),
        P("lat", "lon"),
        P(),
        P("segment", None, None),
        P("segment", None, None),
        P("segment", None, None),
        P("segment", None, None),
        P("segment", None, None),
        P("segment", None, None),
        P("segment", None, None),
        P("segment", None, None),
        P("segment", None, None, None),
    )
    out_specs = P("segment", None, "lat", "lon", None, None)
    return jax.shard_map(body, mesh=mesh, in_specs=in_specs, out_specs=out_specs, check_vma=False)
```

```python
import functools

import jax
import jax.numpy as jnp
from jax import lax
from jax.experimental import pallas as pl
from jax.experimental.pallas import tpu as pltpu
from jax.sharding import PartitionSpec as P

epsilon = 1e-05


def layer_norm(values, gain_row):
    mean_val = jnp.mean(values, axis=-1, keepdims=True)
    centered = values - mean_val
    variance = jnp.mean(centered * centered, axis=-1, keepdims=True)
    return centered * lax.rsqrt(variance + epsilon) * gain_row


def lat_halo(array, width):
    devices, length = lax.axis_size("lat"), array.shape[1]
    up = [(i, i + 1) for i in range(devices - 1)]
    down = [(j, i) for i, j in up]
    before = lax.ppermute(array[:, length - width :], "lat", up)
    after = lax.ppermute(array[:, :width], "lat", down)
    return jnp.concatenate([before, array, after], axis=1)


def head_bias(bias_segment, groups, lon_total, levels):
    heads_here = bias_segment.shape[0] // groups
    group = lax.axis_index("lon") // (lax.axis_size("lon") // groups)
    picked = lax.dynamic_slice_in_dim(bias_segment, group * heads_here, heads_here, axis=0)
    lhs = picked.reshape(heads_here * levels, lon_total)
    high = lhs.astype(jnp.bfloat16)
    rest = lhs - high.astype(jnp.float32)
    middle = rest.astype(jnp.bfloat16)
    low = (rest - middle.astype(jnp.float32)).astype(jnp.bfloat16)
    lon = jnp.arange(lon_total, dtype=jnp.int32)
    key_lon = jnp.repeat(lon, levels)
    offsets = jnp.mod(key_lon[None, :] - lon[:, None], lon_total)
    onehot = (lon[:, None, None] == offsets[None]).astype(jnp.bfloat16).reshape(lon_total, -1)
    parts = [
        jnp.dot(part, onehot, preferred_element_type=jnp.float32) for part in (high, middle, low)
    ]
    table = (parts[0] + parts[1]) + parts[2]
    table = table.reshape(heads_here, levels, lon_total, lon_total * levels)
    table = jnp.transpose(table, (0, 2, 1, 3))
    return table.reshape(heads_here, lon_total * levels, lon_total * levels)


def attention_kernel(x_ref, bias_ref, o_ref, *, heads, head_dim):
    width = heads * head_dim
    step = pl.program_id(0)
    for h in range(heads):

        @pl.when(step == h)
        def _():
            cols = slice(h * head_dim, (h + 1) * head_dim)
            q = x_ref[:, cols]
            k = x_ref[:, width + h * head_dim : width + (h + 1) * head_dim]
            v = x_ref[:, 2 * width + h * head_dim : 2 * width + (h + 1) * head_dim]
            s = lax.dot_general(q, k, (((1,), (1,)), ((), ())), preferred_element_type=jnp.float32)
            s = s * (head_dim ** (-0.5)) + bias_ref[0]
            row_max = jnp.max(s, axis=-1, keepdims=True)
            weights = jnp.exp(s - row_max)
            total = jnp.sum(weights, axis=-1, keepdims=True)
            summed = jnp.dot(weights.astype(jnp.bfloat16), v, preferred_element_type=jnp.float32)
            o_ref[:, cols] = (summed / total).astype(o_ref.dtype)


def attend(x, bias_full, head_dim):
    heads, queries, keys = bias_full.shape
    return pl.pallas_call(
        functools.partial(attention_kernel, heads=heads, head_dim=head_dim),
        out_shape=jax.ShapeDtypeStruct((x.shape[0], heads * head_dim), jnp.bfloat16),
        grid=(heads,),
        in_specs=[
            pl.BlockSpec(x.shape, lambda h: (0, 0)),
            pl.BlockSpec((1, queries, keys), lambda h: (h, 0, 0)),
        ],
        out_specs=pl.BlockSpec((x.shape[0], heads * head_dim), lambda h: (0, 0)),
    )(x, bias_full)


def block(field, lead_index, mask_ids, params, bias_full):
    mask_tab, lead_tab, wqkv, wout, wup, wdown, gains, taps = params
    members, rows_lat, lon_local, levels, features = field.shape
    groups, _, group_width = wqkv.shape
    heads_here = bias_full.shape[0]
    head_dim = group_width // (3 * heads_here)
    lon_devices = lax.axis_size("lon")
    tokens_local = lon_local * levels
    combos = members * rows_lat

    kinds = mask_tab.shape[0]
    mask_onehot = (mask_ids[..., None] == jnp.arange(kinds, dtype=jnp.int32)).astype(jnp.float32)
    mask_embed = jnp.dot(mask_onehot, mask_tab, precision=lax.Precision.HIGHEST)
    lead_row = lax.dynamic_index_in_dim(lead_tab, lead_index, axis=0, keepdims=False)
    hidden = field + mask_embed[None, :, :, None, :] + lead_row
    normed = layer_norm(hidden, gains[0]).astype(jnp.bfloat16)
    spread = jnp.broadcast_to(normed.reshape(1, -1, features), (groups, combos * tokens_local, features))
    projected = jnp.einsum(
        "gnc,gcf->gnf", spread, wqkv, preferred_element_type=jnp.float32
    ).astype(jnp.bfloat16)
    outgoing = projected.reshape(lon_devices, tokens_local, group_width)
    incoming = lax.all_to_all(outgoing, "lon", 0, 0, tiled=True)
    attended = attend(incoming.reshape(lon_devices * tokens_local, group_width), bias_full, head_dim)
    back = attended.reshape(lon_devices, tokens_local, heads_here * head_dim)
    returned = lax.all_to_all(back, "lon", 0, 0, tiled=True)
    returned = returned.reshape(groups, combos * tokens_local, heads_here * head_dim)
    projected_out = jnp.einsum("gnf,gfo->no", returned, wout, preferred_element_type=jnp.float32)
    hidden2 = hidden + projected_out.reshape(hidden.shape)
    normed2 = layer_norm(hidden2, gains[1]).astype(jnp.bfloat16)
    padded = lat_halo(normed2, 2)
    window_sum = jnp.zeros_like(hidden2)
    for offset_row in range(5):
        window_sum = window_sum + taps[offset_row] * padded[:, offset_row : offset_row + rows_lat].astype(
            jnp.float32
        )
    hidden3 = hidden2 + window_sum
    normed3 = layer_norm(hidden3, gains[2]).astype(jnp.bfloat16)
    activated = jax.nn.gelu(
        jnp.dot(normed3.reshape(-1, features), wup, preferred_element_type=jnp.float32),
        approximate=True,
    ).astype(jnp.bfloat16)
    return hidden3 + jnp.dot(activated, wdown, preferred_element_type=jnp.float32).reshape(hidden.shape)


def from_partner(array):
    return lax.ppermute(array, "segment", [(i, i ^ 1) for i in range(lax.axis_size("segment"))])


def body(
    initial_state,
    mask_ids,
    lead_steps,
    mask_table,
    lead_table,
    w_qkv,
    w_out,
    w_up,
    w_down,
    norm_gains,
    merid_taps,
    score_bias,
):
    members, rows_lat = initial_state.shape[0], initial_state.shape[1]
    lon_local = initial_state.shape[2]
    lon_devices = lax.axis_size("lon")
    head_count = score_bias.shape[1]
    groups = lon_devices // (members * rows_lat)
    mask_tab, lead_tab, wqkv, wout, wup, wdown, gains, taps = tuple(
        item[0] for item in (mask_table, lead_table, w_qkv, w_out, w_up, w_down, norm_gains, merid_taps)
    )
    features = wqkv.shape[0]
    head_dim = features // head_count
    heads_here = head_count // groups
    wqkv = jnp.transpose(wqkv.reshape(features, 3, groups, heads_here * head_dim), (2, 0, 1, 3))
    wqkv = wqkv.reshape(groups, features, 3 * heads_here * head_dim)
    wout = wout.reshape(groups, heads_here * head_dim, features)
    params = (mask_tab, lead_tab, wqkv, wout, wup, wdown, gains, taps)
    bias_full = head_bias(score_bias[0], groups, lon_local * lon_devices, initial_state.shape[3])
    segment_first = lax.axis_index("segment") == 0
    current = initial_state
    first = None
    for tick_num in range(4):
        result = block(current, lead_steps[tick_num // 2], mask_ids, params, bias_full)
        if tick_num == 3:
            break
        current = from_partner(result)
        if tick_num == 1:
            first = current
    output = jnp.where(segment_first, first, result)
    return output[None]


def solution(mesh):
    in_specs = (
        P(None, "lat", "lon", None, None),
        P("lat", "lon"),
        P(),
        P("segment", None, None),
        P("segment", None, None),
        P("segment", None, None),
        P("segment", None, None),
        P("segment", None, None),
        P("segment", None, None),
        P("segment", None, None),
        P("segment", None, None),
        P("segment", None, None, None),
    )
    out_specs = P("segment", None, "lat", "lon", None, None)
    return jax.shard_map(body, mesh=mesh, in_specs=in_specs, out_specs=out_specs, check_vma=False)
```

```python
import functools

import jax
import numpy as np
import jax.numpy as jnp
from jax import lax
from jax.experimental import pallas as pl
from jax.experimental.pallas import tpu as pltpu
from jax.sharding import PartitionSpec as P

epsilon = 1e-05


def layer_norm(values, gain_row):
    mean_val = jnp.mean(values, axis=-1, keepdims=True)
    centered = values - mean_val
    variance = jnp.mean(centered * centered, axis=-1, keepdims=True)
    return centered * lax.rsqrt(variance + epsilon) * gain_row


def lat_halo(array, width):
    devices, length = lax.axis_size("lat"), array.shape[1]
    up = [(i, i + 1) for i in range(devices - 1)]
    down = [(j, i) for i, j in up]
    before = lax.ppermute(array[:, length - width :], "lat", up)
    after = lax.ppermute(array[:, :width], "lat", down)
    return jnp.concatenate([before, array, after], axis=1)


def head_bias(bias_segment, groups, lon_total, levels):
    heads_here = bias_segment.shape[0] // groups
    group = lax.axis_index("lon") // (lax.axis_size("lon") // groups)
    picked = lax.dynamic_slice_in_dim(bias_segment, group * heads_here, heads_here, axis=0)
    lhs = picked.reshape(heads_here * levels, lon_total)
    high = lhs.astype(jnp.bfloat16)
    rest = lhs - high.astype(jnp.float32)
    middle = rest.astype(jnp.bfloat16)
    low = (rest - middle.astype(jnp.float32)).astype(jnp.bfloat16)
    lon = jnp.arange(lon_total, dtype=jnp.int32)
    key_lon = jnp.repeat(lon, levels)
    offsets = jnp.mod(key_lon[None, :] - lon[:, None], lon_total)
    onehot = (lon[:, None, None] == offsets[None]).astype(jnp.bfloat16).reshape(lon_total, -1)
    parts = [
        jnp.dot(part, onehot, preferred_element_type=jnp.float32) for part in (high, middle, low)
    ]
    table = (parts[0] + parts[1]) + parts[2]
    table = table.reshape(heads_here, levels, lon_total, lon_total * levels)
    table = jnp.transpose(table, (0, 2, 1, 3))
    return table.reshape(heads_here, lon_total * levels, lon_total * levels)


def attention_kernel(x_ref, bias_ref, o_ref, *, heads, head_dim):
    width = heads * head_dim
    for h in range(heads):
        cols = slice(h * head_dim, (h + 1) * head_dim)
        q = x_ref[:, cols]
        k = x_ref[:, width + h * head_dim : width + (h + 1) * head_dim]
        v = x_ref[:, 2 * width + h * head_dim : 2 * width + (h + 1) * head_dim]
        s = lax.dot_general(q, k, (((1,), (1,)), ((), ())), preferred_element_type=jnp.float32)
        s = s * (head_dim ** (-0.5)) + bias_ref[h]
        row_max = jnp.max(s, axis=-1, keepdims=True)
        weights = jnp.exp(s - row_max)
        total = jnp.sum(weights, axis=-1, keepdims=True)
        summed = jnp.dot(weights.astype(jnp.bfloat16), v, preferred_element_type=jnp.float32)
        o_ref[:, cols] = (summed / total).astype(o_ref.dtype)


def attend(x, bias_full, head_dim):
    heads = bias_full.shape[0]
    return pl.pallas_call(
        functools.partial(attention_kernel, heads=heads, head_dim=head_dim),
        out_shape=jax.ShapeDtypeStruct((x.shape[0], heads * head_dim), jnp.bfloat16),
        in_specs=[pl.BlockSpec(memory_space=pltpu.VMEM)] * 2,
        out_specs=pl.BlockSpec(memory_space=pltpu.VMEM),
    )(x, bias_full)


def tail_kernel(h2_ref, pad_ref, taps_ref, gain_ref, wup_ref, wdown_ref, o_ref, h3_ref):
    members, rows_lat, tokens, features = h2_ref.shape
    taps = taps_ref[...]
    for m in range(members):
        for r in range(rows_lat):
            window_sum = jnp.zeros((tokens, features), jnp.float32)
            for k in range(taps.shape[0]):
                window_sum = window_sum + taps[k : k + 1] * pad_ref[m, r + k].astype(jnp.float32)
            start = (m * rows_lat + r) * tokens
            h3_ref[start : start + tokens, :] = h2_ref[m, r] + window_sum
    hidden3 = h3_ref[...]
    mean_val = jnp.mean(hidden3, axis=-1, keepdims=True)
    centered = hidden3 - mean_val
    variance = jnp.mean(centered * centered, axis=-1, keepdims=True)
    normed3 = (centered * lax.rsqrt(variance + epsilon) * gain_ref[...]).astype(jnp.bfloat16)
    up = jnp.dot(normed3, wup_ref[...], preferred_element_type=jnp.float32)
    cdf = 0.5 * (1.0 + jnp.tanh(np.sqrt(2 / np.pi).astype(np.float32) * (up + 0.044715 * (up * up * up))))
    activated = (up * cdf).astype(jnp.bfloat16)
    o_ref[...] = hidden3 + jnp.dot(activated, wdown_ref[...], preferred_element_type=jnp.float32)


def block_tail(hidden2, padded, taps, gain_row, wup, wdown):
    members, rows_lat = hidden2.shape[0], hidden2.shape[1]
    features = hidden2.shape[-1]
    h2 = hidden2.reshape(members, rows_lat, -1, features)
    pad = padded.reshape(members, padded.shape[1], -1, features)
    count = members * rows_lat * h2.shape[2]
    vmem = pl.BlockSpec(memory_space=pltpu.VMEM)
    out = pl.pallas_call(
        tail_kernel,
        out_shape=jax.ShapeDtypeStruct((count, features), jnp.float32),
        in_specs=[vmem] * 6,
        out_specs=vmem,
        scratch_shapes=[pltpu.VMEM((count, features), jnp.float32)],
    )(h2, pad, taps, gain_row.reshape(1, features), wup, wdown)
    return out.reshape(hidden2.shape)


def block(field, lead_index, mask_ids, params, bias_full):
    mask_tab, lead_tab, wqkv, wout, wup, wdown, gains, taps = params
    members, rows_lat, lon_local, levels, features = field.shape
    groups, _, group_width = wqkv.shape
    heads_here = bias_full.shape[0]
    head_dim = group_width // (3 * heads_here)
    lon_devices = lax.axis_size("lon")
    tokens_local = lon_local * levels
    combos = members * rows_lat

    mask_embed = jnp.take(mask_tab, mask_ids, axis=0)
    lead_row = lax.dynamic_index_in_dim(lead_tab, lead_index, axis=0, keepdims=False)
    hidden = field + mask_embed[None, :, :, None, :] + lead_row
    normed = layer_norm(hidden, gains[0]).astype(jnp.bfloat16)
    spread = jnp.broadcast_to(normed.reshape(1, -1, features), (groups, combos * tokens_local, features))
    projected = jnp.einsum(
        "gnc,gcf->gnf", spread, wqkv, preferred_element_type=jnp.float32
    ).astype(jnp.bfloat16)
    outgoing = projected.reshape(lon_devices, tokens_local, group_width)
    incoming = lax.all_to_all(outgoing, "lon", 0, 0, tiled=True)
    attended = attend(incoming.reshape(lon_devices * tokens_local, group_width), bias_full, head_dim)
    back = attended.reshape(lon_devices, tokens_local, heads_here * head_dim)
    returned = lax.all_to_all(back, "lon", 0, 0, tiled=True)
    returned = returned.reshape(groups, combos * tokens_local, heads_here * head_dim)
    projected_out = jnp.einsum("gnf,gfo->no", returned, wout, preferred_element_type=jnp.float32)
    hidden2 = hidden + projected_out.reshape(hidden.shape)
    normed2 = layer_norm(hidden2, gains[1]).astype(jnp.bfloat16)
    padded = lat_halo(normed2, 2)
    return block_tail(hidden2, padded, taps, gains[2], wup, wdown)


def from_partner(array):
    return lax.ppermute(array, "segment", [(i, i ^ 1) for i in range(lax.axis_size("segment"))])


def body(
    initial_state,
    mask_ids,
    lead_steps,
    mask_table,
    lead_table,
    w_qkv,
    w_out,
    w_up,
    w_down,
    norm_gains,
    merid_taps,
    score_bias,
):
    members, rows_lat = initial_state.shape[0], initial_state.shape[1]
    lon_local = initial_state.shape[2]
    lon_devices = lax.axis_size("lon")
    head_count = score_bias.shape[1]
    groups = lon_devices // (members * rows_lat)
    mask_tab, lead_tab, wqkv, wout, wup, wdown, gains, taps = tuple(
        item[0] for item in (mask_table, lead_table, w_qkv, w_out, w_up, w_down, norm_gains, merid_taps)
    )
    features = wqkv.shape[0]
    head_dim = features // head_count
    heads_here = head_count // groups
    wqkv = jnp.transpose(wqkv.reshape(features, 3, groups, heads_here * head_dim), (2, 0, 1, 3))
    wqkv = wqkv.reshape(groups, features, 3 * heads_here * head_dim)
    wout = wout.reshape(groups, heads_here * head_dim, features)
    params = (mask_tab, lead_tab, wqkv, wout, wup, wdown, gains, taps)
    bias_full = head_bias(score_bias[0], groups, lon_local * lon_devices, initial_state.shape[3])
    segment_first = lax.axis_index("segment") == 0
    current = initial_state
    first = None
    for tick_num in range(4):
        result = block(current, lead_steps[tick_num // 2], mask_ids, params, bias_full)
        if tick_num == 3:
            break
        current = from_partner(result)
        if tick_num == 1:
            first = current
    output = jnp.where(segment_first, first, result)
    return output[None]


def solution(mesh):
    in_specs = (
        P(None, "lat", "lon", None, None),
        P("lat", "lon"),
        P(),
        P("segment", None, None),
        P("segment", None, None),
        P("segment", None, None),
        P("segment", None, None),
        P("segment", None, None),
        P("segment", None, None),
        P("segment", None, None),
        P("segment", None, None),
        P("segment", None, None, None),
    )
    out_specs = P("segment", None, "lat", "lon", None, None)
    return jax.shard_map(body, mesh=mesh, in_specs=in_specs, out_specs=out_specs, check_vma=False)
```

```python
import functools

import jax
import jax.numpy as jnp
from jax import lax
from jax.experimental import pallas as pl
from jax.experimental.pallas import tpu as pltpu
from jax.sharding import PartitionSpec as P

epsilon = 1e-05


def layer_norm(values, gain_row):
    mean_val = jnp.mean(values, axis=-1, keepdims=True)
    centered = values - mean_val
    variance = jnp.mean(centered * centered, axis=-1, keepdims=True)
    return centered * lax.rsqrt(variance + epsilon) * gain_row


def lat_halo(array, width):
    devices, length = lax.axis_size("lat"), array.shape[1]
    up = [(i, i + 1) for i in range(devices - 1)]
    down = [(j, i) for i, j in up]
    before = lax.ppermute(array[:, length - width :], "lat", up)
    after = lax.ppermute(array[:, :width], "lat", down)
    return jnp.concatenate([before, array, after], axis=1)


def head_bias(bias_segment, groups, lon_total, levels):
    heads_here = bias_segment.shape[0] // groups
    group = lax.axis_index("lon") // (lax.axis_size("lon") // groups)
    picked = lax.dynamic_slice_in_dim(bias_segment, group * heads_here, heads_here, axis=0)
    lhs = picked.reshape(heads_here * levels, lon_total)
    high = lhs.astype(jnp.bfloat16)
    rest = lhs - high.astype(jnp.float32)
    middle = rest.astype(jnp.bfloat16)
    low = (rest - middle.astype(jnp.float32)).astype(jnp.bfloat16)
    lon = jnp.arange(lon_total, dtype=jnp.int32)
    key_lon = jnp.repeat(lon, levels)
    offsets = jnp.mod(key_lon[None, :] - lon[:, None], lon_total)
    onehot = (lon[:, None, None] == offsets[None]).astype(jnp.bfloat16).reshape(lon_total, -1)
    parts = [
        jnp.dot(part, onehot, preferred_element_type=jnp.float32) for part in (high, middle, low)
    ]
    table = (parts[0] + parts[1]) + parts[2]
    table = table.reshape(heads_here, levels, lon_total, lon_total * levels)
    table = jnp.transpose(table, (0, 2, 1, 3))
    return table.reshape(heads_here, lon_total * levels, lon_total * levels)


def attention_kernel(x_ref, bias_ref, o_ref, *, heads, head_dim):
    width = heads * head_dim
    for h in range(heads):
        cols = slice(h * head_dim, (h + 1) * head_dim)
        q = x_ref[:, cols]
        k = x_ref[:, width + h * head_dim : width + (h + 1) * head_dim]
        v = x_ref[:, 2 * width + h * head_dim : 2 * width + (h + 1) * head_dim]
        s = lax.dot_general(q, k, (((1,), (1,)), ((), ())), preferred_element_type=jnp.float32)
        s = s * (head_dim ** (-0.5)) + bias_ref[h]
        row_max = jnp.max(s, axis=-1, keepdims=True)
        weights = jnp.exp(s - row_max)
        total = jnp.sum(weights, axis=-1, keepdims=True)
        summed = jnp.dot(weights.astype(jnp.bfloat16), v, preferred_element_type=jnp.float32)
        o_ref[:, cols] = (summed / total).astype(o_ref.dtype)


def attend(x, bias_full, head_dim):
    heads = bias_full.shape[0]
    return pl.pallas_call(
        functools.partial(attention_kernel, heads=heads, head_dim=head_dim),
        out_shape=jax.ShapeDtypeStruct((x.shape[0], heads * head_dim), jnp.bfloat16),
        in_specs=[pl.BlockSpec(memory_space=pltpu.VMEM)] * 2,
        out_specs=pl.BlockSpec(memory_space=pltpu.VMEM),
    )(x, bias_full)


def block(field, lead_index, mask_ids, params, bias_full):
    mask_tab, lead_tab, wqkv, wout, wup, wdown, gains, taps = params
    members, rows_lat, lon_local, levels, features = field.shape
    groups, _, group_width = wqkv.shape
    heads_here = bias_full.shape[0]
    head_dim = group_width // (3 * heads_here)
    lon_devices = lax.axis_size("lon")
    tokens_local = lon_local * levels
    combos = members * rows_lat

    kinds = mask_tab.shape[0]
    mask_onehot = (mask_ids[..., None] == jnp.arange(kinds, dtype=jnp.int32)).astype(jnp.float32)
    mask_embed = jnp.dot(mask_onehot, mask_tab, precision=lax.Precision.HIGHEST)
    lead_row = lax.dynamic_index_in_dim(lead_tab, lead_index, axis=0, keepdims=False)
    hidden = field + mask_embed[None, :, :, None, :] + lead_row
    normed = layer_norm(hidden, gains[0]).astype(jnp.bfloat16)
    spread = jnp.broadcast_to(normed.reshape(1, -1, features), (groups, combos * tokens_local, features))
    projected = jnp.einsum(
        "gnc,gcf->gnf", spread, wqkv, preferred_element_type=jnp.float32
    ).astype(jnp.bfloat16)
    outgoing = projected.reshape(lon_devices, tokens_local, group_width)
    incoming = lax.all_to_all(outgoing, "lon", 0, 0, tiled=True)
    attended = attend(incoming.reshape(lon_devices * tokens_local, group_width), bias_full, head_dim)
    back = attended.reshape(lon_devices, tokens_local, heads_here * head_dim)
    returned = lax.all_to_all(back, "lon", 0, 0, tiled=True)
    returned = returned.reshape(groups, combos * tokens_local, heads_here * head_dim)
    projected_out = jnp.einsum("gnf,gfo->no", returned, wout, preferred_element_type=jnp.float32)
    hidden2 = hidden + projected_out.reshape(hidden.shape)
    normed2 = layer_norm(hidden2, gains[1]).astype(jnp.bfloat16)
    padded = lat_halo(normed2, 2)
    window_sum = jnp.zeros_like(hidden2)
    for offset_row in range(5):
        window_sum = window_sum + taps[offset_row] * padded[:, offset_row : offset_row + rows_lat].astype(
            jnp.float32
        )
    hidden3 = hidden2 + window_sum
    normed3 = layer_norm(hidden3, gains[2]).astype(jnp.bfloat16)
    activated = jax.nn.gelu(
        jnp.dot(normed3.reshape(-1, features), wup, preferred_element_type=jnp.float32),
        approximate=True,
    ).astype(jnp.bfloat16)
    return hidden3 + jnp.dot(activated, wdown, preferred_element_type=jnp.float32).reshape(hidden.shape)


def from_partner(array):
    return lax.ppermute(array, "segment", [(i, i ^ 1) for i in range(lax.axis_size("segment"))])


def body(
    initial_state,
    mask_ids,
    lead_steps,
    mask_table,
    lead_table,
    w_qkv,
    w_out,
    w_up,
    w_down,
    norm_gains,
    merid_taps,
    score_bias,
):
    members, rows_lat = initial_state.shape[0], initial_state.shape[1]
    lon_local = initial_state.shape[2]
    lon_devices = lax.axis_size("lon")
    head_count = score_bias.shape[1]
    groups = lon_devices // (members * rows_lat)
    mask_tab, lead_tab, wqkv, wout, wup, wdown, gains, taps = tuple(
        item[0] for item in (mask_table, lead_table, w_qkv, w_out, w_up, w_down, norm_gains, merid_taps)
    )
    features = wqkv.shape[0]
    head_dim = features // head_count
    heads_here = head_count // groups
    wqkv = jnp.transpose(wqkv.reshape(features, 3, groups, heads_here * head_dim), (2, 0, 1, 3))
    wqkv = wqkv.reshape(groups, features, 3 * heads_here * head_dim)
    wout = wout.reshape(groups, heads_here * head_dim, features)
    params = (mask_tab, lead_tab, wqkv, wout, wup, wdown, gains, taps)
    bias_full = head_bias(score_bias[0], groups, lon_local * lon_devices, initial_state.shape[3])
    segment_first = lax.axis_index("segment") == 0
    current = initial_state
    first = None
    for tick_num in range(4):
        result = block(current, lead_steps[tick_num // 2], mask_ids, params, bias_full)
        if tick_num == 3:
            break
        current = from_partner(result)
        if tick_num == 1:
            first = current
    output = jnp.where(segment_first, first, result)
    return output[None]


def solution(mesh):
    in_specs = (
        P(None, "lat", "lon", None, None),
        P("lat", "lon"),
        P(),
        P("segment", None, None),
        P("segment", None, None),
        P("segment", None, None),
        P("segment", None, None),
        P("segment", None, None),
        P("segment", None, None),
        P("segment", None, None),
        P("segment", None, None),
        P("segment", None, None, None),
    )
    out_specs = P("segment", None, "lat", "lon", None, None)
    return jax.shard_map(body, mesh=mesh, in_specs=in_specs, out_specs=out_specs, check_vma=False)
```

```python
import functools

import jax
import jax.numpy as jnp
from jax import lax
from jax.experimental import pallas as pl
from jax.experimental.pallas import tpu as pltpu
from jax.sharding import PartitionSpec as P

epsilon = 1e-05


def layer_norm(values, gain_row):
    mean_val = jnp.mean(values, axis=-1, keepdims=True)
    centered = values - mean_val
    variance = jnp.mean(centered * centered, axis=-1, keepdims=True)
    return centered * lax.rsqrt(variance + epsilon) * gain_row


def lat_halo(array, width):
    devices, length = lax.axis_size("lat"), array.shape[1]
    up = [(i, i + 1) for i in range(devices - 1)]
    down = [(j, i) for i, j in up]
    before = lax.ppermute(array[:, length - width :], "lat", up)
    after = lax.ppermute(array[:, :width], "lat", down)
    return jnp.concatenate([before, array, after], axis=1)


def head_bias(bias_segment, groups, levels):
    heads_here = bias_segment.shape[0] // groups
    group = lax.axis_index("lon") // (lax.axis_size("lon") // groups)
    picked = lax.dynamic_slice_in_dim(bias_segment, group * heads_here, heads_here, axis=0)
    return jnp.repeat(picked, levels, axis=2)


def attention_kernel(x_ref, base_ref, o_ref, bias_ref, *, heads, head_dim, levels):
    width = heads * head_dim
    lon_total = x_ref.shape[0] // levels
    for h in range(heads):
        base = base_ref[h]
        for i in range(lon_total):
            rotated = base if i == 0 else pltpu.roll(base, i * levels, 1)
            bias_ref[h, i * levels : (i + 1) * levels, :] = rotated
    for h in range(heads):
        cols = slice(h * head_dim, (h + 1) * head_dim)
        q = x_ref[:, cols]
        k = x_ref[:, width + h * head_dim : width + (h + 1) * head_dim]
        v = x_ref[:, 2 * width + h * head_dim : 2 * width + (h + 1) * head_dim]
        s = lax.dot_general(q, k, (((1,), (1,)), ((), ())), preferred_element_type=jnp.float32)
        s = s * (head_dim ** (-0.5)) + bias_ref[h]
        row_max = jnp.max(s, axis=-1, keepdims=True)
        weights = jnp.exp(s - row_max)
        total = jnp.sum(weights, axis=-1, keepdims=True)
        summed = jnp.dot(weights.astype(jnp.bfloat16), v, preferred_element_type=jnp.float32)
        o_ref[:, cols] = (summed / total).astype(o_ref.dtype)


def attend(x, bias_base, head_dim):
    heads, levels, keys = bias_base.shape
    return pl.pallas_call(
        functools.partial(attention_kernel, heads=heads, head_dim=head_dim, levels=levels),
        out_shape=jax.ShapeDtypeStruct((x.shape[0], heads * head_dim), jnp.bfloat16),
        in_specs=[pl.BlockSpec(memory_space=pltpu.VMEM)] * 2,
        out_specs=pl.BlockSpec(memory_space=pltpu.VMEM),
        scratch_shapes=[pltpu.VMEM((heads, x.shape[0], keys), jnp.float32)],
    )(x, bias_base)


def block(field, lead_index, mask_ids, params, bias_full):
    mask_tab, lead_tab, wqkv, wout, wup, wdown, gains, taps = params
    members, rows_lat, lon_local, levels, features = field.shape
    groups, _, group_width = wqkv.shape
    heads_here = bias_full.shape[0]
    head_dim = group_width // (3 * heads_here)
    lon_devices = lax.axis_size("lon")
    tokens_local = lon_local * levels
    combos = members * rows_lat

    kinds = mask_tab.shape[0]
    mask_onehot = (mask_ids[..., None] == jnp.arange(kinds, dtype=jnp.int32)).astype(jnp.float32)
    mask_embed = jnp.dot(mask_onehot, mask_tab, precision=lax.Precision.HIGHEST)
    lead_row = lax.dynamic_index_in_dim(lead_tab, lead_index, axis=0, keepdims=False)
    hidden = field + mask_embed[None, :, :, None, :] + lead_row
    normed = layer_norm(hidden, gains[0]).astype(jnp.bfloat16)
    spread = jnp.broadcast_to(normed.reshape(1, -1, features), (groups, combos * tokens_local, features))
    projected = jnp.einsum(
        "gnc,gcf->gnf", spread, wqkv, preferred_element_type=jnp.float32
    ).astype(jnp.bfloat16)
    outgoing = projected.reshape(lon_devices, tokens_local, group_width)
    incoming = lax.all_to_all(outgoing, "lon", 0, 0, tiled=True)
    attended = attend(incoming.reshape(lon_devices * tokens_local, group_width), bias_full, head_dim)
    back = attended.reshape(lon_devices, tokens_local, heads_here * head_dim)
    returned = lax.all_to_all(back, "lon", 0, 0, tiled=True)
    returned = returned.reshape(groups, combos * tokens_local, heads_here * head_dim)
    projected_out = jnp.einsum("gnf,gfo->no", returned, wout, preferred_element_type=jnp.float32)
    hidden2 = hidden + projected_out.reshape(hidden.shape)
    normed2 = layer_norm(hidden2, gains[1]).astype(jnp.bfloat16)
    padded = lat_halo(normed2, 2)
    window_sum = jnp.zeros_like(hidden2)
    for offset_row in range(5):
        window_sum = window_sum + taps[offset_row] * padded[:, offset_row : offset_row + rows_lat].astype(
            jnp.float32
        )
    hidden3 = hidden2 + window_sum
    normed3 = layer_norm(hidden3, gains[2]).astype(jnp.bfloat16)
    activated = jax.nn.gelu(
        jnp.dot(normed3.reshape(-1, features), wup, preferred_element_type=jnp.float32),
        approximate=True,
    ).astype(jnp.bfloat16)
    return hidden3 + jnp.dot(activated, wdown, preferred_element_type=jnp.float32).reshape(hidden.shape)


def from_partner(array):
    return lax.ppermute(array, "segment", [(i, i ^ 1) for i in range(lax.axis_size("segment"))])


def body(
    initial_state,
    mask_ids,
    lead_steps,
    mask_table,
    lead_table,
    w_qkv,
    w_out,
    w_up,
    w_down,
    norm_gains,
    merid_taps,
    score_bias,
):
    members, rows_lat = initial_state.shape[0], initial_state.shape[1]
    lon_local = initial_state.shape[2]
    lon_devices = lax.axis_size("lon")
    head_count = score_bias.shape[1]
    groups = lon_devices // (members * rows_lat)
    mask_tab, lead_tab, wqkv, wout, wup, wdown, gains, taps = tuple(
        item[0] for item in (mask_table, lead_table, w_qkv, w_out, w_up, w_down, norm_gains, merid_taps)
    )
    features = wqkv.shape[0]
    head_dim = features // head_count
    heads_here = head_count // groups
    wqkv = jnp.transpose(wqkv.reshape(features, 3, groups, heads_here * head_dim), (2, 0, 1, 3))
    wqkv = wqkv.reshape(groups, features, 3 * heads_here * head_dim)
    wout = wout.reshape(groups, heads_here * head_dim, features)
    params = (mask_tab, lead_tab, wqkv, wout, wup, wdown, gains, taps)
    bias_full = head_bias(score_bias[0], groups, initial_state.shape[3])
    segment_first = lax.axis_index("segment") == 0
    current = initial_state
    first = None
    for tick_num in range(4):
        result = block(current, lead_steps[tick_num // 2], mask_ids, params, bias_full)
        if tick_num == 3:
            break
        current = from_partner(result)
        if tick_num == 1:
            first = current
    output = jnp.where(segment_first, first, result)
    return output[None]


def solution(mesh):
    in_specs = (
        P(None, "lat", "lon", None, None),
        P("lat", "lon"),
        P(),
        P("segment", None, None),
        P("segment", None, None),
        P("segment", None, None),
        P("segment", None, None),
        P("segment", None, None),
        P("segment", None, None),
        P("segment", None, None),
        P("segment", None, None),
        P("segment", None, None, None),
    )
    out_specs = P("segment", None, "lat", "lon", None, None)
    return jax.shard_map(body, mesh=mesh, in_specs=in_specs, out_specs=out_specs, check_vma=False)
```

```python
import functools

import jax
import jax.numpy as jnp
from jax import lax
from jax.experimental import pallas as pl
from jax.experimental.pallas import tpu as pltpu
from jax.sharding import PartitionSpec as P

epsilon = 1e-05


def layer_norm(values, gain_row):
    mean_val = jnp.mean(values, axis=-1, keepdims=True)
    centered = values - mean_val
    variance = jnp.mean(centered * centered, axis=-1, keepdims=True)
    return centered * lax.rsqrt(variance + epsilon) * gain_row


def lat_halo(array, width):
    devices, length = lax.axis_size("lat"), array.shape[1]
    up = [(i, i + 1) for i in range(devices - 1)]
    down = [(j, i) for i, j in up]
    before = lax.ppermute(array[:, length - width :], "lat", up)
    after = lax.ppermute(array[:, :width], "lat", down)
    return jnp.concatenate([before, array, after], axis=1)


def head_bias(bias_segment, groups, levels):
    heads_here = bias_segment.shape[0] // groups
    group = lax.axis_index("lon") // (lax.axis_size("lon") // groups)
    picked = lax.dynamic_slice_in_dim(bias_segment, group * heads_here, heads_here, axis=0)
    return jnp.repeat(picked, levels, axis=2)


def attention_kernel(x_ref, base_ref, o_ref, bias_ref, *, heads, head_dim, levels):
    width = heads * head_dim
    lon_total = x_ref.shape[0] // levels
    for h in range(heads):
        base = base_ref[h]
        for i in range(lon_total):
            rotated = base if i == 0 else pltpu.roll(base, i * levels, 1)
            bias_ref[h, i * levels : (i + 1) * levels, :] = rotated
    for h in range(heads):
        cols = slice(h * head_dim, (h + 1) * head_dim)
        q = x_ref[:, cols]
        k = x_ref[:, width + h * head_dim : width + (h + 1) * head_dim]
        v = x_ref[:, 2 * width + h * head_dim : 2 * width + (h + 1) * head_dim]
        s = lax.dot_general(q, k, (((1,), (1,)), ((), ())), preferred_element_type=jnp.float32)
        s = s * (head_dim ** (-0.5)) + bias_ref[h]
        row_max = jnp.max(s, axis=-1, keepdims=True)
        weights = jnp.exp(s - row_max)
        total = jnp.sum(weights, axis=-1, keepdims=True)
        summed = jnp.dot(weights.astype(jnp.bfloat16), v, preferred_element_type=jnp.float32)
        o_ref[:, cols] = (summed / total).astype(o_ref.dtype)


def attend(x, bias_base, head_dim):
    heads, levels, keys = bias_base.shape
    return pl.pallas_call(
        functools.partial(attention_kernel, heads=heads, head_dim=head_dim, levels=levels),
        out_shape=jax.ShapeDtypeStruct((x.shape[0], heads * head_dim), jnp.bfloat16),
        in_specs=[pl.BlockSpec(memory_space=pltpu.VMEM)] * 2,
        out_specs=pl.BlockSpec(memory_space=pltpu.VMEM),
        scratch_shapes=[pltpu.VMEM((heads, x.shape[0], keys), jnp.float32)],
    )(x, bias_base)


def block(field, lead_index, mask_ids, params, bias_full):
    mask_tab, lead_tab, wqkv, wout, wup, wdown, gains, taps = params
    members, rows_lat, lon_local, levels, features = field.shape
    groups = wout.shape[0]
    group_width = wqkv.shape[1] // groups
    heads_here = bias_full.shape[0]
    head_dim = group_width // (3 * heads_here)
    lon_devices = lax.axis_size("lon")
    tokens_local = lon_local * levels
    combos = members * rows_lat

    kinds = mask_tab.shape[0]
    mask_onehot = (mask_ids[..., None] == jnp.arange(kinds, dtype=jnp.int32)).astype(jnp.float32)
    mask_embed = jnp.dot(mask_onehot, mask_tab, precision=lax.Precision.HIGHEST)
    lead_row = lax.dynamic_index_in_dim(lead_tab, lead_index, axis=0, keepdims=False)
    hidden = field + mask_embed[None, :, :, None, :] + lead_row
    normed = layer_norm(hidden, gains[0]).astype(jnp.bfloat16)
    projected = jnp.dot(
        normed.reshape(-1, features), wqkv, preferred_element_type=jnp.float32
    ).astype(jnp.bfloat16)
    projected = projected.reshape(combos * tokens_local, 3, groups, group_width // 3)
    outgoing = jnp.transpose(projected, (2, 0, 1, 3)).reshape(lon_devices, tokens_local, group_width)
    incoming = lax.all_to_all(outgoing, "lon", 0, 0, tiled=True)
    attended = attend(incoming.reshape(lon_devices * tokens_local, group_width), bias_full, head_dim)
    back = attended.reshape(lon_devices, tokens_local, heads_here * head_dim)
    returned = lax.all_to_all(back, "lon", 0, 0, tiled=True)
    returned = returned.reshape(groups, combos * tokens_local, heads_here * head_dim)
    projected_out = jnp.einsum("gnf,gfo->no", returned, wout, preferred_element_type=jnp.float32)
    hidden2 = hidden + projected_out.reshape(hidden.shape)
    normed2 = layer_norm(hidden2, gains[1]).astype(jnp.bfloat16)
    padded = lat_halo(normed2, 2)
    window_sum = jnp.zeros_like(hidden2)
    for offset_row in range(5):
        window_sum = window_sum + taps[offset_row] * padded[:, offset_row : offset_row + rows_lat].astype(
            jnp.float32
        )
    hidden3 = hidden2 + window_sum
    normed3 = layer_norm(hidden3, gains[2]).astype(jnp.bfloat16)
    activated = jax.nn.gelu(
        jnp.dot(normed3.reshape(-1, features), wup, preferred_element_type=jnp.float32),
        approximate=True,
    ).astype(jnp.bfloat16)
    return hidden3 + jnp.dot(activated, wdown, preferred_element_type=jnp.float32).reshape(hidden.shape)


def from_partner(array):
    return lax.ppermute(array, "segment", [(i, i ^ 1) for i in range(lax.axis_size("segment"))])


def body(
    initial_state,
    mask_ids,
    lead_steps,
    mask_table,
    lead_table,
    w_qkv,
    w_out,
    w_up,
    w_down,
    norm_gains,
    merid_taps,
    score_bias,
):
    members, rows_lat = initial_state.shape[0], initial_state.shape[1]
    lon_local = initial_state.shape[2]
    lon_devices = lax.axis_size("lon")
    head_count = score_bias.shape[1]
    groups = lon_devices // (members * rows_lat)
    mask_tab, lead_tab, wqkv, wout, wup, wdown, gains, taps = tuple(
        item[0] for item in (mask_table, lead_table, w_qkv, w_out, w_up, w_down, norm_gains, merid_taps)
    )
    features = wqkv.shape[0]
    head_dim = features // head_count
    heads_here = head_count // groups
    wout = wout.reshape(groups, heads_here * head_dim, features)
    params = (mask_tab, lead_tab, wqkv, wout, wup, wdown, gains, taps)
    bias_full = head_bias(score_bias[0], groups, initial_state.shape[3])
    segment_first = lax.axis_index("segment") == 0
    current = initial_state
    first = None
    for tick_num in range(4):
        result = block(current, lead_steps[tick_num // 2], mask_ids, params, bias_full)
        if tick_num == 3:
            break
        current = from_partner(result)
        if tick_num == 1:
            first = current
    output = jnp.where(segment_first, first, result)
    return output[None]


def solution(mesh):
    in_specs = (
        P(None, "lat", "lon", None, None),
        P("lat", "lon"),
        P(),
        P("segment", None, None),
        P("segment", None, None),
        P("segment", None, None),
        P("segment", None, None),
        P("segment", None, None),
        P("segment", None, None),
        P("segment", None, None),
        P("segment", None, None),
        P("segment", None, None, None),
    )
    out_specs = P("segment", None, "lat", "lon", None, None)
    return jax.shard_map(body, mesh=mesh, in_specs=in_specs, out_specs=out_specs, check_vma=False)
```

```python
import functools

import jax
import jax.numpy as jnp
from jax import lax
from jax.experimental import pallas as pl
from jax.experimental.pallas import tpu as pltpu
from jax.sharding import PartitionSpec as P

epsilon = 1e-05


def layer_norm(values, gain_row):
    mean_val = jnp.mean(values, axis=-1, keepdims=True)
    centered = values - mean_val
    variance = jnp.mean(centered * centered, axis=-1, keepdims=True)
    return centered * lax.rsqrt(variance + epsilon) * gain_row


def lat_halo(array, width):
    devices, length = lax.axis_size("lat"), array.shape[1]
    up = [(i, i + 1) for i in range(devices - 1)]
    down = [(j, i) for i, j in up]
    before = lax.ppermute(array[:, length - width :], "lat", up)
    after = lax.ppermute(array[:, :width], "lat", down)
    return jnp.concatenate([before, array, after], axis=1)


def head_bias(bias_segment, groups, levels):
    heads_here = bias_segment.shape[0] // groups
    group = lax.axis_index("lon") // (lax.axis_size("lon") // groups)
    picked = lax.dynamic_slice_in_dim(bias_segment, group * heads_here, heads_here, axis=0)
    return jnp.repeat(picked, levels, axis=2)


def attention_kernel(x_ref, base_ref, o_ref, bias_ref, *, heads, head_dim, levels):
    width = heads * head_dim
    lon_total = x_ref.shape[0] // levels
    for h in range(heads):
        base = base_ref[h]
        for i in range(lon_total):
            rotated = base if i == 0 else pltpu.roll(base, i * levels, 1)
            bias_ref[h, i * levels : (i + 1) * levels, :] = rotated
    for h in range(heads):
        cols = slice(h * head_dim, (h + 1) * head_dim)
        q = x_ref[:, cols]
        k = x_ref[:, width + h * head_dim : width + (h + 1) * head_dim]
        v = x_ref[:, 2 * width + h * head_dim : 2 * width + (h + 1) * head_dim]
        s = lax.dot_general(q, k, (((1,), (1,)), ((), ())), preferred_element_type=jnp.float32)
        s = s * (head_dim ** (-0.5)) + bias_ref[h]
        row_max = jnp.max(s, axis=-1, keepdims=True)
        weights = jnp.exp(s - row_max)
        total = jnp.sum(weights, axis=-1, keepdims=True)
        summed = jnp.dot(weights.astype(jnp.bfloat16), v, preferred_element_type=jnp.float32)
        o_ref[:, cols] = (summed / total).astype(o_ref.dtype)


def attend(x, bias_base, head_dim):
    heads, levels, keys = bias_base.shape
    return pl.pallas_call(
        functools.partial(attention_kernel, heads=heads, head_dim=head_dim, levels=levels),
        out_shape=jax.ShapeDtypeStruct((x.shape[0], heads * head_dim), jnp.bfloat16),
        in_specs=[pl.BlockSpec(memory_space=pltpu.VMEM)] * 2,
        out_specs=pl.BlockSpec(memory_space=pltpu.VMEM),
        scratch_shapes=[pltpu.VMEM((heads, x.shape[0], keys), jnp.float32)],
    )(x, bias_base)


def block(field, lead_index, mask_ids, params, bias_full):
    mask_tab, lead_tab, wqkv, wout, wup, wdown, gains, taps = params
    members, rows_lat, lon_local, levels, features = field.shape
    groups, _, group_width = wqkv.shape
    heads_here = bias_full.shape[0]
    head_dim = group_width // (3 * heads_here)
    lon_devices = lax.axis_size("lon")
    tokens_local = lon_local * levels
    combos = members * rows_lat

    kinds = mask_tab.shape[0]
    mask_onehot = (mask_ids[..., None] == jnp.arange(kinds, dtype=jnp.int32)).astype(jnp.float32)
    mask_embed = jnp.dot(mask_onehot, mask_tab, precision=lax.Precision.HIGHEST)
    lead_row = lax.dynamic_index_in_dim(lead_tab, lead_index, axis=0, keepdims=False)
    hidden = field + mask_embed[None, :, :, None, :] + lead_row
    normed = layer_norm(hidden, gains[0]).astype(jnp.bfloat16)
    spread = jnp.broadcast_to(normed.reshape(1, -1, features), (groups, combos * tokens_local, features))
    projected = jnp.einsum(
        "gnc,gcf->gnf", spread, wqkv, preferred_element_type=jnp.float32
    ).astype(jnp.bfloat16)
    outgoing = projected.reshape(lon_devices, tokens_local, group_width)
    incoming = lax.all_to_all(outgoing, "lon", 0, 0, tiled=True)
    attended = attend(incoming.reshape(lon_devices * tokens_local, group_width), bias_full, head_dim)
    back = attended.reshape(lon_devices, tokens_local, heads_here * head_dim)
    returned = lax.all_to_all(back, "lon", 0, 0, tiled=True)
    returned = returned.reshape(groups, combos * tokens_local, heads_here * head_dim)
    projected_out = jnp.einsum("gnf,gfo->no", returned, wout, preferred_element_type=jnp.float32)
    hidden2 = hidden + projected_out.reshape(hidden.shape)
    normed2 = layer_norm(hidden2, gains[1]).astype(jnp.bfloat16)
    padded = lat_halo(normed2, 2)
    window_sum = jnp.zeros_like(hidden2)
    for offset_row in range(5):
        window_sum = window_sum + taps[offset_row] * padded[:, offset_row : offset_row + rows_lat].astype(
            jnp.float32
        )
    hidden3 = hidden2 + window_sum
    normed3 = layer_norm(hidden3, gains[2]).astype(jnp.bfloat16)
    activated = jax.nn.gelu(
        jnp.dot(normed3.reshape(-1, features), wup, preferred_element_type=jnp.float32),
        approximate=True,
    ).astype(jnp.bfloat16)
    return hidden3 + jnp.dot(activated, wdown, preferred_element_type=jnp.float32).reshape(hidden.shape)


def from_partner(array):
    return lax.ppermute(array, "segment", [(i, i ^ 1) for i in range(lax.axis_size("segment"))])


def body(
    initial_state,
    mask_ids,
    lead_steps,
    mask_table,
    lead_table,
    w_qkv,
    w_out,
    w_up,
    w_down,
    norm_gains,
    merid_taps,
    score_bias,
):
    members, rows_lat = initial_state.shape[0], initial_state.shape[1]
    lon_local = initial_state.shape[2]
    lon_devices = lax.axis_size("lon")
    head_count = score_bias.shape[1]
    groups = lon_devices // (members * rows_lat)
    mask_tab, lead_tab, wqkv, wout, wup, wdown, gains, taps = tuple(
        item[0] for item in (mask_table, lead_table, w_qkv, w_out, w_up, w_down, norm_gains, merid_taps)
    )
    features = wqkv.shape[0]
    head_dim = features // head_count
    heads_here = head_count // groups
    wqkv = jnp.transpose(wqkv.reshape(features, 3, groups, heads_here * head_dim), (2, 0, 1, 3))
    wqkv = wqkv.reshape(groups, features, 3 * heads_here * head_dim)
    wout = wout.reshape(groups, heads_here * head_dim, features)
    params = (mask_tab, lead_tab, wqkv, wout, wup, wdown, gains, taps)
    bias_full = head_bias(score_bias[0], groups, initial_state.shape[3])
    segment_first = lax.axis_index("segment") == 0
    current = initial_state
    first = None
    for tick_num in range(4):
        result = block(current, lead_steps[tick_num // 2], mask_ids, params, bias_full)
        if tick_num == 3:
            break
        current = from_partner(result.astype(jnp.bfloat16)).astype(result.dtype)
        if tick_num == 1:
            first = current
    output = jnp.where(segment_first, first, result)
    return output[None]


def solution(mesh):
    in_specs = (
        P(None, "lat", "lon", None, None),
        P("lat", "lon"),
        P(),
        P("segment", None, None),
        P("segment", None, None),
        P("segment", None, None),
        P("segment", None, None),
        P("segment", None, None),
        P("segment", None, None),
        P("segment", None, None),
        P("segment", None, None),
        P("segment", None, None, None),
    )
    out_specs = P("segment", None, "lat", "lon", None, None)
    return jax.shard_map(body, mesh=mesh, in_specs=in_specs, out_specs=out_specs, check_vma=False)
```

```python
import functools

import jax
import jax.numpy as jnp
from jax import lax
from jax.experimental import pallas as pl
from jax.experimental.pallas import tpu as pltpu
from jax.sharding import PartitionSpec as P

epsilon = 1e-05


def layer_norm(values, gain_row):
    mean_val = jnp.mean(values, axis=-1, keepdims=True)
    centered = values - mean_val
    variance = jnp.mean(centered * centered, axis=-1, keepdims=True)
    return centered * lax.rsqrt(variance + epsilon) * gain_row


def lat_halo(array, width):
    devices, length = lax.axis_size("lat"), array.shape[1]
    up = [(i, i + 1) for i in range(devices - 1)]
    down = [(j, i) for i, j in up]
    before = lax.ppermute(array[:, length - width :], "lat", up)
    after = lax.ppermute(array[:, :width], "lat", down)
    return jnp.concatenate([before, array, after], axis=1)


def head_bias(bias_segment, groups, levels):
    heads_here = bias_segment.shape[0] // groups
    group = lax.axis_index("lon") // (lax.axis_size("lon") // groups)
    picked = lax.dynamic_slice_in_dim(bias_segment, group * heads_here, heads_here, axis=0)
    return jnp.repeat(picked, levels, axis=2)


def attention_kernel(x_ref, base_ref, o_ref, *, heads, head_dim, levels, chunk):
    width = heads * head_dim
    lon_total = x_ref.shape[0] // levels
    for h in range(heads):
        base = base_ref[h]
        k = x_ref[:, width + h * head_dim : width + (h + 1) * head_dim]
        v = x_ref[:, 2 * width + h * head_dim : 2 * width + (h + 1) * head_dim]
        for start in range(0, lon_total, chunk):
            rows = slice(start * levels, (start + chunk) * levels)
            cols = slice(h * head_dim, (h + 1) * head_dim)
            bias = jnp.concatenate(
                [base if i == 0 else pltpu.roll(base, i * levels, 1) for i in range(start, start + chunk)],
                axis=0,
            )
            q = x_ref[rows, cols]
            s = lax.dot_general(q, k, (((1,), (1,)), ((), ())), preferred_element_type=jnp.float32)
            s = s * (head_dim ** (-0.5)) + bias
            row_max = jnp.max(s, axis=-1, keepdims=True)
            weights = jnp.exp(s - row_max)
            total = jnp.sum(weights, axis=-1, keepdims=True)
            summed = jnp.dot(weights.astype(jnp.bfloat16), v, preferred_element_type=jnp.float32)
            o_ref[rows, cols] = (summed / total).astype(o_ref.dtype)


def attend(x, bias_base, head_dim):
    heads, levels, keys = bias_base.shape
    return pl.pallas_call(
        functools.partial(attention_kernel, heads=heads, head_dim=head_dim, levels=levels, chunk=8),
        out_shape=jax.ShapeDtypeStruct((x.shape[0], heads * head_dim), jnp.bfloat16),
        in_specs=[pl.BlockSpec(memory_space=pltpu.VMEM)] * 2,
        out_specs=pl.BlockSpec(memory_space=pltpu.VMEM),
    )(x, bias_base)


def block(field, lead_index, mask_ids, params, bias_full):
    mask_tab, lead_tab, wqkv, wout, wup, wdown, gains, taps = params
    members, rows_lat, lon_local, levels, features = field.shape
    groups, _, group_width = wqkv.shape
    heads_here = bias_full.shape[0]
    head_dim = group_width // (3 * heads_here)
    lon_devices = lax.axis_size("lon")
    tokens_local = lon_local * levels
    combos = members * rows_lat

    kinds = mask_tab.shape[0]
    mask_onehot = (mask_ids[..., None] == jnp.arange(kinds, dtype=jnp.int32)).astype(jnp.float32)
    mask_embed = jnp.dot(mask_onehot, mask_tab, precision=lax.Precision.HIGHEST)
    lead_row = lax.dynamic_index_in_dim(lead_tab, lead_index, axis=0, keepdims=False)
    hidden = field + mask_embed[None, :, :, None, :] + lead_row
    normed = layer_norm(hidden, gains[0]).astype(jnp.bfloat16)
    spread = jnp.broadcast_to(normed.reshape(1, -1, features), (groups, combos * tokens_local, features))
    projected = jnp.einsum(
        "gnc,gcf->gnf", spread, wqkv, preferred_element_type=jnp.float32
    ).astype(jnp.bfloat16)
    outgoing = projected.reshape(lon_devices, tokens_local, group_width)
    incoming = lax.all_to_all(outgoing, "lon", 0, 0, tiled=True)
    attended = attend(incoming.reshape(lon_devices * tokens_local, group_width), bias_full, head_dim)
    back = attended.reshape(lon_devices, tokens_local, heads_here * head_dim)
    returned = lax.all_to_all(back, "lon", 0, 0, tiled=True)
    returned = returned.reshape(groups, combos * tokens_local, heads_here * head_dim)
    projected_out = jnp.einsum("gnf,gfo->no", returned, wout, preferred_element_type=jnp.float32)
    hidden2 = hidden + projected_out.reshape(hidden.shape)
    normed2 = layer_norm(hidden2, gains[1]).astype(jnp.bfloat16)
    padded = lat_halo(normed2, 2)
    window_sum = jnp.zeros_like(hidden2)
    for offset_row in range(5):
        window_sum = window_sum + taps[offset_row] * padded[:, offset_row : offset_row + rows_lat].astype(
            jnp.float32
        )
    hidden3 = hidden2 + window_sum
    normed3 = layer_norm(hidden3, gains[2]).astype(jnp.bfloat16)
    activated = jax.nn.gelu(
        jnp.dot(normed3.reshape(-1, features), wup, preferred_element_type=jnp.float32),
        approximate=True,
    ).astype(jnp.bfloat16)
    return hidden3 + jnp.dot(activated, wdown, preferred_element_type=jnp.float32).reshape(hidden.shape)


def from_partner(array):
    return lax.ppermute(array, "segment", [(i, i ^ 1) for i in range(lax.axis_size("segment"))])


def body(
    initial_state,
    mask_ids,
    lead_steps,
    mask_table,
    lead_table,
    w_qkv,
    w_out,
    w_up,
    w_down,
    norm_gains,
    merid_taps,
    score_bias,
):
    members, rows_lat = initial_state.shape[0], initial_state.shape[1]
    lon_local = initial_state.shape[2]
    lon_devices = lax.axis_size("lon")
    head_count = score_bias.shape[1]
    groups = lon_devices // (members * rows_lat)
    mask_tab, lead_tab, wqkv, wout, wup, wdown, gains, taps = tuple(
        item[0] for item in (mask_table, lead_table, w_qkv, w_out, w_up, w_down, norm_gains, merid_taps)
    )
    features = wqkv.shape[0]
    head_dim = features // head_count
    heads_here = head_count // groups
    wqkv = jnp.transpose(wqkv.reshape(features, 3, groups, heads_here * head_dim), (2, 0, 1, 3))
    wqkv = wqkv.reshape(groups, features, 3 * heads_here * head_dim)
    wout = wout.reshape(groups, heads_here * head_dim, features)
    params = (mask_tab, lead_tab, wqkv, wout, wup, wdown, gains, taps)
    bias_full = head_bias(score_bias[0], groups, initial_state.shape[3])
    segment_first = lax.axis_index("segment") == 0
    current = initial_state
    first = None
    for tick_num in range(4):
        result = block(current, lead_steps[tick_num // 2], mask_ids, params, bias_full)
        if tick_num == 3:
            break
        current = from_partner(result.astype(jnp.bfloat16)).astype(result.dtype)
        if tick_num == 1:
            first = current
    output = jnp.where(segment_first, first, result)
    return output[None]


def solution(mesh):
    in_specs = (
        P(None, "lat", "lon", None, None),
        P("lat", "lon"),
        P(),
        P("segment", None, None),
        P("segment", None, None),
        P("segment", None, None),
        P("segment", None, None),
        P("segment", None, None),
        P("segment", None, None),
        P("segment", None, None),
        P("segment", None, None),
        P("segment", None, None, None),
    )
    out_specs = P("segment", None, "lat", "lon", None, None)
    return jax.shard_map(body, mesh=mesh, in_specs=in_specs, out_specs=out_specs, check_vma=False)
```
